256 devices in a mesh: seq: 32 (over x, y, core), exp: 8 (over z).
Axes of the slice: x: 4, y: 4, z: 8, core: 2. Of those that a mesh axis runs over, the one named last changes fastest.
Arguments:
- query_rows: bfloat16 [2048, 8192], P('seq', 'exp'), may hold values from -6 to 6
- key_rows: bfloat16 [2048, 8192], P('seq', 'exp'), may hold values from -6 to 6
- value_rows: bfloat16 [2048, 8192], P('seq', 'exp'), may hold values from -120 to 120
- log_decay: float32 [2048, 64], P('seq', 'exp'), may hold values from -1.4625 to 0, as said below
- out_weight: bfloat16 [8192, 6144], P('exp', 'seq'), may hold values from -0.0625 to 0.0625
- residual: bfloat16 [2048, 6144], P('exp', 'seq'), may hold values from -18 to 18
- routes: int32 [2048, 2], P('exp'), may hold values from 0 to 7, all different within a row; in each aligned block of 256 rows (0 to 255, 256 to 511, ...) at most 128 rows name the same one
- gate_weight: bfloat16 [8, 9216, 6144], P('exp', 'seq'), may hold values from -0.078125 to 0.078125
- up_weight: bfloat16 [8, 9216, 6144], P('exp', 'seq'), may hold values from -0.078125 to 0.078125
Outputs:
- residual_out: bfloat16 [2048, 6144], P('exp', 'seq')
- expert_hidden: bfloat16 [8, 9216, 1024], P('exp', 'seq')
The draws below stay inside these ranges and needn't reach their ends.
Inputs may be any that keep to these rules, and one draw needn't show every extreme that they name: `routes`: each token names 2 different experts; within one source group of 256 tokens no expert is named more than 128 times. `log_decay`: every entry is negative.
All inputs are finite; a program needn't handle non-finite values.
Results may differ from the reference program's by a relative error of at most 0.0065.
Values may be sent and summed in bfloat16 or wider, within the bound.
No kernel may reach another device: no remote copies, remote signals or barrier semaphores. Data moves between devices by JAX's collectives and lax.ppermute only.
A program may use at most 128 MiB of HBM per device.

```python
import math
import jax
import jax.numpy as jnp
import numpy as np
from jax import lax

D = 6144
HEADS = 64
HEAD_DIM = 128
FF = 9216
TOP = 2
TOK_SEQ = 64
SEQUENCE_LENGTH = 2048
EXPERTS = 8
BLOCK = 256
CAP = 128


def draw_log_decay(key, part):
    selection_key, quick_decay_key, gradual_decay_key, block_random_key, noise_random_key, spike_random_key, decay_depth_key = jax.random.split(key, 7)
    fast_share = 5
    fast_heads = jax.random.randint(selection_key, (HEADS,), 0, 10) < fast_share
    fast_rate = jnp.exp(jax.random.uniform(quick_decay_key, (HEADS,), jnp.float32, math.log(1.5), math.log(2.5))) / TOK_SEQ
    slow_rate = jax.random.uniform(gradual_decay_key, (HEADS,), jnp.float32, 0.05, 0.2) / SEQUENCE_LENGTH
    baseline_decay_rate = jnp.where(fast_heads, fast_rate, slow_rate)
    blocks_total = SEQUENCE_LENGTH // TOK_SEQ
    block_scale_factor = jnp.exp(jax.random.uniform(block_random_key, (blocks_total, 1, HEADS), jnp.float32, math.log(0.5), 0.0))
    block_scale_factor = jnp.broadcast_to(block_scale_factor, (blocks_total, TOK_SEQ, HEADS)).reshape(SEQUENCE_LENGTH, HEADS)
    random_noise = jax.random.uniform(noise_random_key, (SEQUENCE_LENGTH, HEADS), jnp.float32, 0.5, 1.5)
    spike_positions = jax.random.randint(spike_random_key, (2,), 0, SEQUENCE_LENGTH)
    decay_depth = jax.random.uniform(decay_depth_key, (2, HEADS), jnp.float32, 0.22, 0.69)
    spikes_inserted = (jnp.arange(SEQUENCE_LENGTH)[:, None] == spike_positions[None, :]).astype(jnp.float32)
    spike_values = jnp.sum(spikes_inserted[:, :, None] * decay_depth[None, :, :], axis=1)
    decay_rate = baseline_decay_rate[None, :] * block_scale_factor * random_noise + spike_values
    return -decay_rate


def draw_value_rows(key, part):
    normal_key = jax.random.fold_in(key, 0)
    columns = HEADS * HEAD_DIM
    base = jnp.clip(jax.random.normal(normal_key, (SEQUENCE_LENGTH, columns), jnp.float32), -6.0, 6.0)
    return base.astype(jnp.bfloat16)


def draw_residual(key, part):
    normal_key = jax.random.fold_in(key, 0)
    base = jnp.clip(jax.random.normal(normal_key, (SEQUENCE_LENGTH, D), jnp.float32), -6.0, 6.0)
    return base.astype(jnp.bfloat16)


def levels(rng, dims, cuts, smallest, high):
    def one(dim, parts):
        steps = jax.random.uniform(jax.random.fold_in(jax.random.fold_in(rng, 6), dim), (parts,), jnp.float32, smallest / len(cuts), high / len(cuts))
        return jnp.repeat(jnp.exp(steps), dims[dim] // parts).reshape((-1,) + (1,) * (len(dims) - dim - 1))

    factor_of = one(*cuts[0])
    for cut in cuts[1:]:
        factor_of = factor_of * one(*cut)
    return factor_of


def routed_block(own_key, own, number, rows, number_of, top, most, lean):
    sequence = jax.random.permutation(own_key, number_of)
    heavy_load, usual = load_shares(number_of, rows * top, most, lean, True), load_shares(number_of, rows * top, most, lean, False)
    places = jnp.arange(number_of)

    def named(sizes, turn):
        used = int((sizes > 0).sum())
        fixed = max(1, used // 4)
        shifted = fixed + (places - fixed + turn * (used - fixed)) % max(1, number_of - fixed)
        return jnp.zeros((number_of,), jnp.int32).at[sequence[jnp.where(places < fixed, places, shifted)]].set(jnp.asarray(sizes, jnp.int32))

    sizes = jnp.where(number % 4 == 0, named(heavy_load, number // 4), named(usual, number - number // 4 - 1))
    mixed = jax.random.permutation(jax.random.fold_in(own, 3), number_of)
    source_of, taker = mixed[0:number_of // 2 * 2:2], mixed[1:number_of // 2 * 2:2]
    room = jnp.minimum(sizes[source_of] - 1, most - sizes[taker]) // 2
    room = jnp.where((source_of == sequence[0]) | (taker == sequence[0]) | (sizes[taker] == 0), 0, jnp.maximum(room, 0))
    shifted = jax.random.randint(jax.random.fold_in(own, 4), (number_of // 2,), 0, 1 << 20) % (room + 1)
    sizes = sizes.at[source_of].add(-shifted).at[taker].add(shifted)
    members = jnp.searchsorted(jnp.cumsum(sizes), jnp.arange(rows * top), side="right").astype(jnp.int32)
    table = members.reshape(top, rows).T
    table = table[jax.random.permutation(jax.random.fold_in(own, 1), rows)]
    turn = jax.random.randint(jax.random.fold_in(own, 2), (rows, 1), 0, top)
    return jnp.take_along_axis(table, (jnp.arange(top)[None, :] + turn) % top, axis=1)


def load_shares(amount, total, reach, lean, full):
    loads = [(1 << 20) // math.isqrt(rank ** lean) + 1 for rank in range(1, amount + 1)]
    largest = reach if full else min(reach, max(-(-total // amount), total * loads[0] // sum(loads)))
    least = 1 if total - largest >= amount - 1 else 0
    given, rest = [largest] + [least] * (amount - 1), total - largest - least * (amount - 1)
    while rest > 0:
        free = [i for i in range(1, amount) if given[i] < largest] or [i for i in range(1, amount) if given[i] < reach]
        mass, remaining = sum([loads[i] for i in free]), rest
        for i in free:
            addition = min(reach - given[i], max(1, remaining * loads[i] // mass), rest)
            given[i] = given[i] + addition
            rest = rest - addition
    return np.array(given)


def noise(stream_key, dims, scale, bound, cuts=(), dtype=jnp.bfloat16):
    entries = scale * jax.random.normal(stream_key, dims, jnp.float32)
    if cuts:
        entries = entries * levels(stream_key, dims, cuts, -0.22, 0.18)
    return jnp.clip(entries, -bound, bound).astype(dtype)


def setup_inputs(seed: int = 0) -> dict:
    seeds = jax.random.split(jax.random.key(seed), 10)
    query_rows = noise(seeds[0], (SEQUENCE_LENGTH, HEADS * HEAD_DIM), 1.0, 6.0, ((0, 32), (1, 8)))
    key_rows = noise(seeds[1], (SEQUENCE_LENGTH, HEADS * HEAD_DIM), 1.0, 6.0, ((0, 32), (1, 8)))
    value_rows = draw_value_rows(jax.random.fold_in(seeds[9], 71), 0)
    log_decay = draw_log_decay(jax.random.fold_in(seeds[9], 71), 0)
    out_weight = noise(seeds[4], (HEADS * HEAD_DIM, D), (HEADS * HEAD_DIM) ** -0.5, 0.0625, ((0, 8), (1, 32)))
    residual = draw_residual(jax.random.fold_in(seeds[9], 71), 0)
    routes_keys = jax.random.split(jax.random.fold_in(seeds[6], 1), SEQUENCE_LENGTH // BLOCK)
    routes_turns = jax.random.permutation(jax.random.fold_in(seeds[6], 3), SEQUENCE_LENGTH // BLOCK)
    routes = jax.vmap(lambda own, number: routed_block(jax.random.fold_in(seeds[6], 2), own, number, BLOCK, EXPERTS, TOP, CAP, 2))(routes_keys, routes_turns).reshape((SEQUENCE_LENGTH, TOP))
    gate_weight = noise(seeds[7], (EXPERTS, FF, D), D ** -0.5, 0.078125, ((0, 8), (1, 32)))
    up_weight = noise(seeds[8], (EXPERTS, FF, D), D ** -0.5, 0.078125, ((0, 8), (1, 32)))
    return dict(query_rows=query_rows, key_rows=key_rows, value_rows=value_rows, log_decay=log_decay, out_weight=out_weight, residual=residual, routes=routes, gate_weight=gate_weight, up_weight=up_weight)


precise = lax.Precision.HIGHEST

def attention_blocks(query_rows, key_rows, value_rows, log_decay):
    blocks_total = SEQUENCE_LENGTH // TOK_SEQ
    queries = query_rows.astype(jnp.float32).reshape(blocks_total, TOK_SEQ, HEADS, HEAD_DIM)
    keys_all = key_rows.astype(jnp.float32).reshape(blocks_total, TOK_SEQ, HEADS, HEAD_DIM)
    values_all = value_rows.astype(jnp.float32).reshape(blocks_total, TOK_SEQ, HEADS, HEAD_DIM)
    decays = log_decay.reshape(blocks_total, TOK_SEQ, HEADS)
    later = lax.broadcasted_iota(jnp.int32, (TOK_SEQ, TOK_SEQ), 0)
    earlier = lax.broadcasted_iota(jnp.int32, (TOK_SEQ, TOK_SEQ), 1)
    causal = (later >= earlier)[None]

    def advance(carried_state, inputs):
        query_block, key_block, value_block, decay_block = inputs
        cumulative = jnp.cumsum(decay_block, axis=0)
        closing = cumulative[-1]
        carried = jnp.einsum('thd,hde->the', query_block * jnp.exp(cumulative)[:, :, None], carried_state, precision=precise)
        scores = jnp.einsum('thd,shd->hts', query_block, key_block, precision=precise)
        spread = cumulative.T[:, :, None] - cumulative.T[:, None, :]
        weights = jnp.where(causal, jnp.exp(jnp.where(causal, spread, 0.0)), 0.0)
        within = jnp.einsum('hts,she->the', scores * weights, value_block, precision=precise)
        key_scaled = key_block * jnp.exp(closing[None, :] - cumulative)[:, :, None]
        updated = jnp.exp(closing)[:, None, None] * carried_state + jnp.einsum('shd,she->hde', key_scaled, value_block, precision=precise)
        return (updated, carried + within)
    start_state = jnp.zeros((HEADS, HEAD_DIM, HEAD_DIM), jnp.float32)
    _, head_raw = lax.scan(advance, start_state, (queries, keys_all, values_all, decays))
    return head_raw.reshape(SEQUENCE_LENGTH, HEADS, HEAD_DIM)

def reference(query_rows, key_rows, value_rows, log_decay, out_weight, residual, routes, gate_weight, up_weight):
    head_raw = attention_blocks(query_rows, key_rows, value_rows, log_decay)
    normed = head_raw * lax.rsqrt(lax.optimization_barrier(jnp.mean(head_raw * head_raw, axis=-1, keepdims=True)) + 1e-06)
    normed = normed.astype(jnp.bfloat16).reshape(SEQUENCE_LENGTH, HEADS * HEAD_DIM)
    residual_out = (residual.astype(jnp.float32) + jnp.dot(normed, out_weight, preferred_element_type=jnp.float32)).astype(jnp.bfloat16)
    route_flat = routes.reshape(EXPERTS, BLOCK * TOP).astype(jnp.int32)
    expert_ids = jnp.arange(EXPERTS).astype(jnp.int32)
    onehot = (route_flat[:, :, None] == expert_ids[None, None, :]).astype(jnp.int32)
    slot_index = lax.optimization_barrier(jnp.sum(jnp.cumsum(onehot, axis=1) * onehot, axis=2)) - 1
    group_ids = expert_ids[:, None]
    target = (route_flat * (EXPERTS * CAP) + group_ids * CAP + slot_index).astype(jnp.int32)
    source_rows = jnp.repeat(residual_out.reshape(EXPERTS, BLOCK, D), TOP, axis=1)
    dispatched = jnp.zeros((EXPERTS * EXPERTS * CAP, D), jnp.bfloat16)
    dispatched = dispatched.at[target.reshape(-1)].set(source_rows.reshape(-1, D))
    dispatched = dispatched.reshape(EXPERTS, EXPERTS * CAP, D)

    def expert(inputs):
        row_block, gate_part, up_part = inputs
        squares = jnp.einsum('rd,rd->r', row_block, row_block, preferred_element_type=jnp.float32)
        inv_rms = lax.rsqrt(squares / D + 1e-06)[None, :]
        contract = (((1,), (1,)), ((), ()))
        gate_sum = lax.dot_general(gate_part, row_block, contract, preferred_element_type=jnp.float32) * inv_rms
        up_sum = lax.dot_general(up_part, row_block, contract, preferred_element_type=jnp.float32) * inv_rms
        return (jax.nn.silu(gate_sum) * up_sum).astype(jnp.bfloat16)
    expert_hidden = lax.map(expert, (dispatched, gate_weight, up_weight))
    return (residual_out, expert_hidden)
```

```python
import jax
import jax.numpy as jnp
from jax import lax
from jax.sharding import Mesh
from jax.sharding import PartitionSpec as P

D = 6144
HEAD_DIM = 128
SEQ = ("seq_0", "seq_1", "seq_2")


precise = lax.Precision.HIGHEST
contract_last = (((1,), (1,)), ((), ()))


def nothing_yet(shard, identity):
    return jax.tree.map(
        lambda a, e: jnp.broadcast_to(jnp.asarray(e, a.dtype), a.shape), shard, identity
    )


def carried_in(shard, axes, combine, identity):
    before = start = nothing_yet(shard, identity)
    so_far = shard
    for axis in reversed(axes):
        peers, place = (lax.axis_size(axis), lax.axis_index(axis))
        pieces = jax.tree.map(lambda part: lax.all_gather(part, axis), so_far)
        inside, so_far = (start, start)
        for k in range(peers):
            passed = k < place
            so_far = combine(so_far, jax.tree.map(lambda part: part[k], pieces))
            inside = jax.tree.map(lambda new, old: jnp.where(passed, new, old), so_far, inside)
        before = combine(inside, before)
    return before


def link_states(earlier, later):
    return (earlier[0] * later[0], later[0][:, None, None] * earlier[1] + later[1])


def swap_cores(tree):
    return jax.tree.map(lambda part: lax.ppermute(part, "seq_2", [(0, 1), (1, 0)]), tree)


def prefix_over(own, axis):
    peers, place = (lax.axis_size(axis), lax.axis_index(axis))
    shifted = [own] + [
        jax.tree.map(
            lambda part: lax.ppermute(part, axis, [(i, (i + d) % peers) for i in range(peers)]), own
        )
        for d in range(1, peers)
    ]
    start = nothing_yet(own, (1.0, 0.0))
    before, total = (start, start)
    for k in range(peers):
        lag = (place - k) % peers
        piece = jax.tree.map(
            lambda *opts: jnp.select([lag == d for d in range(peers)], opts), *shifted
        )
        total = link_states(total, piece)
        passed = k < place
        before = jax.tree.map(lambda new, old: jnp.where(passed, new, old), total, before)
    return before, total


def entering_state(decay, state):
    core = lax.axis_index("seq_2")
    other = swap_cores((decay, state))
    first = jax.tree.map(lambda mine, theirs: jnp.where(core == 0, mine, theirs), (decay, state), other)
    second = jax.tree.map(lambda mine, theirs: jnp.where(core == 0, theirs, mine), (decay, state), other)
    chip = link_states(first, second)
    half = decay.shape[0] // 2
    mine = jax.tree.map(lambda part: lax.dynamic_slice_in_dim(part, core * half, half, 0), chip)
    along_y, row = prefix_over(mine, "seq_1")
    along_x, _ = prefix_over(row, "seq_0")
    chip_before = link_states(along_x, along_y)
    theirs = swap_cores(chip_before)
    whole = jax.tree.map(
        lambda a, b: jnp.where(core == 0, jnp.concatenate([a, b], 0), jnp.concatenate([b, a], 0)),
        chip_before,
        theirs,
    )
    return jnp.where(core == 0, whole[1], first[0][:, None, None] * whole[1] + first[1])


def finish_rows(gate_sum, up_sum, squares):
    inv_rms = lax.rsqrt(squares / D + 1e-06)[None, :]
    return (jax.nn.silu(gate_sum * inv_rms) * (up_sum * inv_rms)).astype(jnp.bfloat16)


def body(
    query_rows,
    key_rows,
    value_rows,
    log_decay,
    out_weight,
    residual,
    routes,
    gate_weight,
    up_weight,
):
    positions, head_cols = query_rows.shape
    heads_here = head_cols // HEAD_DIM
    queries = query_rows.astype(jnp.float32).reshape(positions, heads_here, HEAD_DIM)
    keys_here = key_rows.astype(jnp.float32).reshape(positions, heads_here, HEAD_DIM)
    values_here = value_rows.astype(jnp.float32).reshape(positions, heads_here, HEAD_DIM)
    cumulative = jnp.cumsum(log_decay, axis=0)
    closing = cumulative[-1]
    key_scaled = keys_here * jnp.exp(closing[None, :] - cumulative)[:, :, None]
    local_state = jnp.einsum("shd,she->hde", key_scaled, values_here, precision=precise)
    entering = entering_state(jnp.exp(closing), local_state)
    later = lax.broadcasted_iota(jnp.int32, (positions, positions), 0)
    earlier = lax.broadcasted_iota(jnp.int32, (positions, positions), 1)
    causal = (later >= earlier)[None]
    carried = jnp.einsum(
        "thd,hde->the", queries * jnp.exp(cumulative)[:, :, None], entering, precision=precise
    )
    scores = jnp.einsum("thd,shd->hts", queries, keys_here, precision=precise)
    spread = cumulative.T[:, :, None] - cumulative.T[:, None, :]
    weights = jnp.where(causal, jnp.exp(jnp.where(causal, spread, 0.0)), 0.0)
    within = jnp.einsum("hts,she->the", scores * weights, values_here, precision=precise)
    head_raw = carried + within
    normed = head_raw * lax.rsqrt(jnp.mean(head_raw * head_raw, axis=-1, keepdims=True) + 1e-06)
    normed = normed.astype(jnp.bfloat16).reshape(positions, head_cols)
    gathered = lax.all_gather(normed, SEQ, axis=0, tiled=True)
    row_block = gathered
    attended = lax.psum_scatter(
        jnp.dot(row_block, out_weight, preferred_element_type=jnp.float32),
        "exp",
        scatter_dimension=0,
        tiled=True,
    )
    residual_out = (residual.astype(jnp.float32) + attended).astype(jnp.bfloat16)
    group_rows = routes.shape[0]
    choices_each = routes.shape[1]
    experts = lax.axis_size("exp")
    capacity = 4 * group_rows // experts
    route_flat = routes.reshape(-1)
    expert_ids = lax.broadcasted_iota(jnp.int32, (1, experts), 1)
    onehot = (route_flat[:, None] == expert_ids).astype(jnp.int32)
    slot_index = jnp.sum(jnp.cumsum(onehot, axis=0) * onehot, axis=1) - 1
    target = route_flat * capacity + slot_index
    w_gate = gate_weight[0]
    w_up = up_weight[0]
    hidden_rows = w_gate.shape[0]
    columns = residual_out.shape[1]
    buffer = jnp.zeros((experts * capacity, columns), jnp.bfloat16)
    buffer = buffer.at[target].set(jnp.repeat(residual_out, choices_each, axis=0))
    received = lax.all_to_all(
        buffer.reshape(experts, capacity, columns), "exp", split_axis=0, concat_axis=0, tiled=True
    )
    sources, entries, gathered_columns = received.shape
    slices = received.reshape(sources * entries, gathered_columns)
    row_block = lax.all_gather(slices, SEQ, axis=1, tiled=True)
    squares = jnp.einsum("rd,rd->r", row_block, row_block, preferred_element_type=jnp.float32)
    gate_sum = lax.dot_general(w_gate, row_block, contract_last, preferred_element_type=jnp.float32)
    up_sum = lax.dot_general(w_up, row_block, contract_last, preferred_element_type=jnp.float32)
    expert_hidden = finish_rows(gate_sum, up_sum, squares).reshape(hidden_rows, sources, entries)
    return (residual_out, expert_hidden.reshape(1, hidden_rows, experts * capacity))


def solution(mesh):
    torus = Mesh(
        mesh.devices.reshape(4, 4, 2, mesh.shape["exp"]), ("seq_0", "seq_1", "seq_2", "exp")
    )
    in_specs = (
        P(SEQ, "exp"),
        P(SEQ, "exp"),
        P(SEQ, "exp"),
        P(SEQ, "exp"),
        P("exp", SEQ),
        P("exp", SEQ),
        P("exp", None),
        P("exp", SEQ, None),
        P("exp", SEQ, None),
    )
    out_specs = (P("exp", SEQ), P("exp", SEQ, None))
    return jax.shard_map(body, mesh=torus, in_specs=in_specs, out_specs=out_specs, check_vma=False)
```

```python
import jax
import jax.numpy as jnp
from jax import lax
from jax.sharding import Mesh
from jax.sharding import PartitionSpec as P

D = 6144
HEAD_DIM = 128
SEQ = ("seq_0", "seq_1", "seq_2")


precise = lax.Precision.HIGHEST
contract_last = (((1,), (1,)), ((), ()))


def nothing_yet(shard, identity):
    return jax.tree.map(
        lambda a, e: jnp.broadcast_to(jnp.asarray(e, a.dtype), a.shape), shard, identity
    )


def carried_in(shard, axes, combine, identity):
    before = start = nothing_yet(shard, identity)
    so_far = shard
    for axis in reversed(axes):
        peers, place = (lax.axis_size(axis), lax.axis_index(axis))
        pieces = jax.tree.map(lambda part: lax.all_gather(part, axis), so_far)
        inside, so_far = (start, start)
        for k in range(peers):
            passed = k < place
            so_far = combine(so_far, jax.tree.map(lambda part: part[k], pieces))
            inside = jax.tree.map(lambda new, old: jnp.where(passed, new, old), so_far, inside)
        before = combine(inside, before)
    return before


def link_states(earlier, later):
    return (earlier[0] * later[0], later[0][:, None, None] * earlier[1] + later[1])


def swap_cores(tree):
    return jax.tree.map(lambda part: lax.ppermute(part, "seq_2", [(0, 1), (1, 0)]), tree)


def prefix_over(own, axis):
    peers, place = (lax.axis_size(axis), lax.axis_index(axis))
    shifted = [own] + [
        jax.tree.map(
            lambda part: lax.ppermute(part, axis, [(i, (i + d) % peers) for i in range(peers)]), own
        )
        for d in range(1, peers)
    ]
    start = nothing_yet(own, (1.0, 0.0))
    before, after = (start, start)
    for d in range(1, peers):
        taken = d <= place
        grown = link_states(shifted[d], before)
        before = jax.tree.map(lambda new, old: jnp.where(taken, new, old), grown, before)
    for d in range(peers - 1, 0, -1):
        taken = d > place
        grown = link_states(after, shifted[d])
        after = jax.tree.map(lambda new, old: jnp.where(taken, new, old), grown, after)
    return before, link_states(link_states(before, own), after)


def entering_state(decay, state):
    core = lax.axis_index("seq_2")
    other = swap_cores((decay, state))
    first = jax.tree.map(lambda mine, theirs: jnp.where(core == 0, mine, theirs), (decay, state), other)
    second = jax.tree.map(lambda mine, theirs: jnp.where(core == 0, theirs, mine), (decay, state), other)
    chip = link_states(first, second)
    half = decay.shape[0] // 2
    mine = jax.tree.map(lambda part: lax.dynamic_slice_in_dim(part, core * half, half, 0), chip)
    along_y, row = prefix_over(mine, "seq_1")
    along_x, _ = prefix_over(row, "seq_0")
    chip_before = link_states(along_x, along_y)
    theirs = swap_cores(chip_before)
    whole = jax.tree.map(
        lambda a, b: jnp.where(core == 0, jnp.concatenate([a, b], 0), jnp.concatenate([b, a], 0)),
        chip_before,
        theirs,
    )
    return jnp.where(core == 0, whole[1], first[0][:, None, None] * whole[1] + first[1])


def finish_rows(gate_sum, up_sum, squares):
    inv_rms = lax.rsqrt(squares / D + 1e-06)[None, :]
    return (jax.nn.silu(gate_sum * inv_rms) * (up_sum * inv_rms)).astype(jnp.bfloat16)


def body(
    query_rows,
    key_rows,
    value_rows,
    log_decay,
    out_weight,
    residual,
    routes,
    gate_weight,
    up_weight,
):
    positions, head_cols = query_rows.shape
    heads_here = head_cols // HEAD_DIM
    queries = query_rows.astype(jnp.float32).reshape(positions, heads_here, HEAD_DIM)
    keys_here = key_rows.astype(jnp.float32).reshape(positions, heads_here, HEAD_DIM)
    values_here = value_rows.astype(jnp.float32).reshape(positions, heads_here, HEAD_DIM)
    cumulative = jnp.cumsum(log_decay, axis=0)
    closing = cumulative[-1]
    key_scaled = keys_here * jnp.exp(closing[None, :] - cumulative)[:, :, None]
    local_state = jnp.einsum("shd,she->hde", key_scaled, values_here, precision=precise)
    entering = entering_state(jnp.exp(closing), local_state)
    later = lax.broadcasted_iota(jnp.int32, (positions, positions), 0)
    earlier = lax.broadcasted_iota(jnp.int32, (positions, positions), 1)
    causal = (later >= earlier)[None]
    carried = jnp.einsum(
        "thd,hde->the", queries * jnp.exp(cumulative)[:, :, None], entering, precision=precise
    )
    scores = jnp.einsum("thd,shd->hts", queries, keys_here, precision=precise)
    spread = cumulative.T[:, :, None] - cumulative.T[:, None, :]
    weights = jnp.where(causal, jnp.exp(jnp.where(causal, spread, 0.0)), 0.0)
    within = jnp.einsum("hts,she->the", scores * weights, values_here, precision=precise)
    head_raw = carried + within
    normed = head_raw * lax.rsqrt(jnp.mean(head_raw * head_raw, axis=-1, keepdims=True) + 1e-06)
    normed = normed.astype(jnp.bfloat16).reshape(positions, head_cols)
    gathered = lax.all_gather(normed, SEQ, axis=0, tiled=True)
    row_block = gathered
    attended = lax.psum_scatter(
        jnp.dot(row_block, out_weight, preferred_element_type=jnp.float32),
        "exp",
        scatter_dimension=0,
        tiled=True,
    )
    residual_out = (residual.astype(jnp.float32) + attended).astype(jnp.bfloat16)
    group_rows = routes.shape[0]
    choices_each = routes.shape[1]
    experts = lax.axis_size("exp")
    capacity = 4 * group_rows // experts
    route_flat = routes.reshape(-1)
    expert_ids = lax.broadcasted_iota(jnp.int32, (1, experts), 1)
    onehot = (route_flat[:, None] == expert_ids).astype(jnp.int32)
    slot_index = jnp.sum(jnp.cumsum(onehot, axis=0) * onehot, axis=1) - 1
    target = route_flat * capacity + slot_index
    w_gate = gate_weight[0]
    w_up = up_weight[0]
    hidden_rows = w_gate.shape[0]
    columns = residual_out.shape[1]
    slots = lax.broadcasted_iota(jnp.int32, (experts * capacity, 1), 0)
    placed = target.reshape(group_rows, choices_each)
    picks = jnp.zeros((experts * capacity, group_rows), jnp.bool_)
    for j in range(choices_each):
        picks = picks | (slots == placed[None, :, j])
    buffer = jnp.dot(
        picks.astype(jnp.bfloat16), residual_out, preferred_element_type=jnp.float32
    ).astype(jnp.bfloat16)
    received = lax.all_to_all(
        buffer.reshape(experts, capacity, columns), "exp", split_axis=0, concat_axis=0, tiled=True
    )
    sources, entries, gathered_columns = received.shape
    slices = received.reshape(sources * entries, gathered_columns)
    row_block = lax.all_gather(slices, SEQ, axis=1, tiled=True)
    squares = jnp.einsum("rd,rd->r", row_block, row_block, preferred_element_type=jnp.float32)
    gate_sum = lax.dot_general(w_gate, row_block, contract_last, preferred_element_type=jnp.float32)
    up_sum = lax.dot_general(w_up, row_block, contract_last, preferred_element_type=jnp.float32)
    expert_hidden = finish_rows(gate_sum, up_sum, squares).reshape(hidden_rows, sources, entries)
    return (residual_out, expert_hidden.reshape(1, hidden_rows, experts * capacity))


def solution(mesh):
    torus = Mesh(
        mesh.devices.reshape(4, 4, 2, mesh.shape["exp"]), ("seq_0", "seq_1", "seq_2", "exp")
    )
    in_specs = (
        P(SEQ, "exp"),
        P(SEQ, "exp"),
        P(SEQ, "exp"),
        P(SEQ, "exp"),
        P("exp", SEQ),
        P("exp", SEQ),
        P("exp", None),
        P("exp", SEQ, None),
        P("exp", SEQ, None),
    )
    out_specs = (P("exp", SEQ), P("exp", SEQ, None))
    return jax.shard_map(body, mesh=torus, in_specs=in_specs, out_specs=out_specs, check_vma=False)
```

```python
import jax
import jax.numpy as jnp
from jax import lax
from jax.sharding import Mesh
from jax.sharding import PartitionSpec as P

D = 6144
HEAD_DIM = 128
SEQ = ("seq_0", "seq_1", "seq_2")


precise = lax.Precision.HIGHEST
contract_last = (((1,), (1,)), ((), ()))


def nothing_yet(shard, identity):
    return jax.tree.map(
        lambda a, e: jnp.broadcast_to(jnp.asarray(e, a.dtype), a.shape), shard, identity
    )


def carried_in(shard, axes, combine, identity):
    before = start = nothing_yet(shard, identity)
    so_far = shard
    for axis in reversed(axes):
        peers, place = (lax.axis_size(axis), lax.axis_index(axis))
        pieces = jax.tree.map(lambda part: lax.all_gather(part, axis), so_far)
        inside, so_far = (start, start)
        for k in range(peers):
            passed = k < place
            so_far = combine(so_far, jax.tree.map(lambda part: part[k], pieces))
            inside = jax.tree.map(lambda new, old: jnp.where(passed, new, old), so_far, inside)
        before = combine(inside, before)
    return before


def link_states(earlier, later):
    return (earlier[0] * later[0], later[0][:, None, None] * earlier[1] + later[1])


def send(pair, axis, perm):
    decay, state = pair
    heads, rows, cols = state.shape
    packed = jnp.concatenate(
        [state, jnp.broadcast_to(decay[:, None, None], (heads, 8, cols))], axis=1
    )
    moved = lax.ppermute(packed, axis, perm)
    return (moved[:, rows, 0], moved[:, :rows])


def swap_cores(pair):
    return send(pair, "seq_2", [(0, 1), (1, 0)])


def ring_sum(part, axis):
    peers = lax.axis_size(axis)
    total = part
    for d in range(1, peers):
        total = total + lax.ppermute(part, axis, [(i, (i + d) % peers) for i in range(peers)])
    return total


def prefix_over(own, axis):
    peers, place = (lax.axis_size(axis), lax.axis_index(axis))
    shifted = [own] + [
        send(own, axis, [(i, (i + d) % peers) for i in range(peers)]) for d in range(1, peers)
    ]
    start = nothing_yet(own, (1.0, 0.0))
    before, after = (start, start)
    for d in range(1, peers):
        taken = d <= place
        grown = link_states(shifted[d], before)
        before = jax.tree.map(lambda new, old: jnp.where(taken, new, old), grown, before)
    for d in range(peers - 1, 0, -1):
        taken = d > place
        grown = link_states(after, shifted[d])
        after = jax.tree.map(lambda new, old: jnp.where(taken, new, old), grown, after)
    return before, link_states(link_states(before, own), after)


def entering_state(decay, state):
    core = lax.axis_index("seq_2")
    other = swap_cores((decay, state))
    first = jax.tree.map(lambda mine, theirs: jnp.where(core == 0, mine, theirs), (decay, state), other)
    second = jax.tree.map(lambda mine, theirs: jnp.where(core == 0, theirs, mine), (decay, state), other)
    chip = link_states(first, second)
    half = decay.shape[0] // 2
    mine = jax.tree.map(lambda part: lax.dynamic_slice_in_dim(part, core * half, half, 0), chip)
    along_y, row = prefix_over(mine, "seq_1")
    along_x, _ = prefix_over(row, "seq_0")
    chip_before = link_states(along_x, along_y)
    theirs = swap_cores(chip_before)
    whole = jax.tree.map(
        lambda a, b: jnp.where(core == 0, jnp.concatenate([a, b], 0), jnp.concatenate([b, a], 0)),
        chip_before,
        theirs,
    )
    return jnp.where(core == 0, whole[1], first[0][:, None, None] * whole[1] + first[1])


def finish_rows(gate_sum, up_sum, squares):
    inv_rms = lax.rsqrt(squares / D + 1e-06)[None, :]
    return (jax.nn.silu(gate_sum * inv_rms) * (up_sum * inv_rms)).astype(jnp.bfloat16)


def body(
    query_rows,
    key_rows,
    value_rows,
    log_decay,
    out_weight,
    residual,
    routes,
    gate_weight,
    up_weight,
):
    positions, head_cols = query_rows.shape
    heads_here = head_cols // HEAD_DIM
    queries = query_rows.astype(jnp.float32).reshape(positions, heads_here, HEAD_DIM)
    keys_here = key_rows.astype(jnp.float32).reshape(positions, heads_here, HEAD_DIM)
    values_here = value_rows.astype(jnp.float32).reshape(positions, heads_here, HEAD_DIM)
    cumulative = jnp.cumsum(log_decay, axis=0)
    closing = cumulative[-1]
    key_scaled = keys_here * jnp.exp(closing[None, :] - cumulative)[:, :, None]
    local_state = jnp.einsum("shd,she->hde", key_scaled, values_here, precision=precise)
    entering = entering_state(jnp.exp(closing), local_state)
    later = lax.broadcasted_iota(jnp.int32, (positions, positions), 0)
    earlier = lax.broadcasted_iota(jnp.int32, (positions, positions), 1)
    causal = (later >= earlier)[None]
    carried = jnp.einsum(
        "thd,hde->the", queries * jnp.exp(cumulative)[:, :, None], entering, precision=precise
    )
    scores = jnp.einsum("thd,shd->hts", queries, keys_here, precision=precise)
    spread = cumulative.T[:, :, None] - cumulative.T[:, None, :]
    weights = jnp.where(causal, jnp.exp(jnp.where(causal, spread, 0.0)), 0.0)
    within = jnp.einsum("hts,she->the", scores * weights, values_here, precision=precise)
    head_raw = carried + within
    normed = head_raw * lax.rsqrt(jnp.mean(head_raw * head_raw, axis=-1, keepdims=True) + 1e-06)
    normed = normed.astype(jnp.bfloat16).reshape(positions, head_cols)
    gathered = lax.all_gather(normed, SEQ, axis=0, tiled=True)
    row_block = gathered
    attended = lax.psum_scatter(
        jnp.dot(row_block, out_weight, preferred_element_type=jnp.float32),
        "exp",
        scatter_dimension=0,
        tiled=True,
    )
    residual_out = (residual.astype(jnp.float32) + attended).astype(jnp.bfloat16)
    group_rows = routes.shape[0]
    choices_each = routes.shape[1]
    experts = lax.axis_size("exp")
    capacity = 4 * group_rows // experts
    route_flat = routes.reshape(-1)
    expert_ids = lax.broadcasted_iota(jnp.int32, (1, experts), 1)
    onehot = (route_flat[:, None] == expert_ids).astype(jnp.int32)
    slot_index = jnp.sum(jnp.cumsum(onehot, axis=0) * onehot, axis=1) - 1
    target = route_flat * capacity + slot_index
    w_gate = gate_weight[0]
    w_up = up_weight[0]
    hidden_rows = w_gate.shape[0]
    columns = residual_out.shape[1]
    slots = lax.broadcasted_iota(jnp.int32, (experts * capacity, 1), 0)
    placed = target.reshape(group_rows, choices_each)
    picks = jnp.zeros((experts * capacity, group_rows), jnp.bool_)
    for j in range(choices_each):
        picks = picks | (slots == placed[None, :, j])
    buffer = jnp.dot(
        picks.astype(jnp.bfloat16), residual_out, preferred_element_type=jnp.float32
    ).astype(jnp.bfloat16)
    received = lax.all_to_all(
        buffer.reshape(experts, capacity, columns), "exp", split_axis=0, concat_axis=0, tiled=True
    )
    sources, entries, gathered_columns = received.shape
    slices = received.reshape(sources * entries, gathered_columns)
    row_block = lax.all_gather(slices, SEQ, axis=1, tiled=True)
    squares = jnp.einsum("rd,rd->r", slices, slices, preferred_element_type=jnp.float32)
    for axis in reversed(SEQ):
        squares = ring_sum(squares, axis)
    gate_sum = lax.dot_general(w_gate, row_block, contract_last, preferred_element_type=jnp.float32)
    up_sum = lax.dot_general(w_up, row_block, contract_last, preferred_element_type=jnp.float32)
    expert_hidden = finish_rows(gate_sum, up_sum, squares).reshape(hidden_rows, sources, entries)
    return (residual_out, expert_hidden.reshape(1, hidden_rows, experts * capacity))


def solution(mesh):
    torus = Mesh(
        mesh.devices.reshape(4, 4, 2, mesh.shape["exp"]), ("seq_0", "seq_1", "seq_2", "exp")
    )
    in_specs = (
        P(SEQ, "exp"),
        P(SEQ, "exp"),
        P(SEQ, "exp"),
        P(SEQ, "exp"),
        P("exp", SEQ),
        P("exp", SEQ),
        P("exp", None),
        P("exp", SEQ, None),
        P("exp", SEQ, None),
    )
    out_specs = (P("exp", SEQ), P("exp", SEQ, None))
    return jax.shard_map(body, mesh=torus, in_specs=in_specs, out_specs=out_specs, check_vma=False)
```

```python
import jax
import jax.numpy as jnp
from jax import lax
from jax.sharding import Mesh
from jax.sharding import PartitionSpec as P

D = 6144
HEAD_DIM = 128
SEQ = ("seq_0", "seq_1", "seq_2")


precise = lax.Precision.HIGHEST
contract_last = (((1,), (1,)), ((), ()))


def nothing_yet(shard, identity):
    return jax.tree.map(
        lambda a, e: jnp.broadcast_to(jnp.asarray(e, a.dtype), a.shape), shard, identity
    )


def carried_in(shard, axes, combine, identity):
    before = start = nothing_yet(shard, identity)
    so_far = shard
    for axis in reversed(axes):
        peers, place = (lax.axis_size(axis), lax.axis_index(axis))
        pieces = jax.tree.map(lambda part: lax.all_gather(part, axis), so_far)
        inside, so_far = (start, start)
        for k in range(peers):
            passed = k < place
            so_far = combine(so_far, jax.tree.map(lambda part: part[k], pieces))
            inside = jax.tree.map(lambda new, old: jnp.where(passed, new, old), so_far, inside)
        before = combine(inside, before)
    return before


def link_states(earlier, later):
    return (earlier[0] * later[0], later[0][:, None, None] * earlier[1] + later[1])


def send(pair, axis, perm):
    decay, state = pair
    moved = lax.ppermute(state.astype(jnp.bfloat16), axis, perm)
    return (lax.ppermute(decay, axis, perm), moved.astype(jnp.float32))


def swap_cores(pair):
    return jax.tree.map(lambda part: lax.ppermute(part, "seq_2", [(0, 1), (1, 0)]), pair)


def ring_sum(part, axis):
    peers = lax.axis_size(axis)
    total = part
    for d in range(1, peers):
        total = total + lax.ppermute(part, axis, [(i, (i + d) % peers) for i in range(peers)])
    return total


def prefix_over(own, axis):
    peers, place = (lax.axis_size(axis), lax.axis_index(axis))
    shifted = [own] + [
        send(own, axis, [(i, (i + d) % peers) for i in range(peers)]) for d in range(1, peers)
    ]
    start = nothing_yet(own, (1.0, 0.0))
    before, after = (start, start)
    for d in range(1, peers):
        taken = d <= place
        grown = link_states(shifted[d], before)
        before = jax.tree.map(lambda new, old: jnp.where(taken, new, old), grown, before)
    for d in range(peers - 1, 0, -1):
        taken = d > place
        grown = link_states(after, shifted[d])
        after = jax.tree.map(lambda new, old: jnp.where(taken, new, old), grown, after)
    return before, link_states(link_states(before, own), after)


def entering_state(decay, state):
    core = lax.axis_index("seq_2")
    other = swap_cores((decay, state))
    first = jax.tree.map(lambda mine, theirs: jnp.where(core == 0, mine, theirs), (decay, state), other)
    second = jax.tree.map(lambda mine, theirs: jnp.where(core == 0, theirs, mine), (decay, state), other)
    chip = link_states(first, second)
    half = decay.shape[0] // 2
    mine = jax.tree.map(lambda part: lax.dynamic_slice_in_dim(part, core * half, half, 0), chip)
    along_y, row = prefix_over(mine, "seq_1")
    along_x, _ = prefix_over(row, "seq_0")
    chip_before = link_states(along_x, along_y)
    theirs = swap_cores(chip_before)
    whole = jax.tree.map(
        lambda a, b: jnp.where(core == 0, jnp.concatenate([a, b], 0), jnp.concatenate([b, a], 0)),
        chip_before,
        theirs,
    )
    return jnp.where(core == 0, whole[1], first[0][:, None, None] * whole[1] + first[1])


def finish_rows(gate_sum, up_sum, squares):
    inv_rms = lax.rsqrt(squares / D + 1e-06)[None, :]
    return (jax.nn.silu(gate_sum * inv_rms) * (up_sum * inv_rms)).astype(jnp.bfloat16)


def body(
    query_rows,
    key_rows,
    value_rows,
    log_decay,
    out_weight,
    residual,
    routes,
    gate_weight,
    up_weight,
):
    positions, head_cols = query_rows.shape
    heads_here = head_cols // HEAD_DIM
    queries = query_rows.astype(jnp.float32).reshape(positions, heads_here, HEAD_DIM)
    keys_here = key_rows.astype(jnp.float32).reshape(positions, heads_here, HEAD_DIM)
    values_here = value_rows.astype(jnp.float32).reshape(positions, heads_here, HEAD_DIM)
    cumulative = jnp.cumsum(log_decay, axis=0)
    closing = cumulative[-1]
    key_scaled = keys_here * jnp.exp(closing[None, :] - cumulative)[:, :, None]
    local_state = jnp.einsum("shd,she->hde", key_scaled, values_here, precision=precise)
    entering = entering_state(jnp.exp(closing), local_state)
    later = lax.broadcasted_iota(jnp.int32, (positions, positions), 0)
    earlier = lax.broadcasted_iota(jnp.int32, (positions, positions), 1)
    causal = (later >= earlier)[None]
    carried = jnp.einsum(
        "thd,hde->the", queries * jnp.exp(cumulative)[:, :, None], entering, precision=precise
    )
    scores = jnp.einsum("thd,shd->hts", queries, keys_here, precision=precise)
    spread = cumulative.T[:, :, None] - cumulative.T[:, None, :]
    weights = jnp.where(causal, jnp.exp(jnp.where(causal, spread, 0.0)), 0.0)
    within = jnp.einsum("hts,she->the", scores * weights, values_here, precision=precise)
    head_raw = carried + within
    normed = head_raw * lax.rsqrt(jnp.mean(head_raw * head_raw, axis=-1, keepdims=True) + 1e-06)
    normed = normed.astype(jnp.bfloat16).reshape(positions, head_cols)
    gathered = lax.all_gather(normed, SEQ, axis=0, tiled=True)
    row_block = gathered
    attended = lax.psum_scatter(
        jnp.dot(row_block, out_weight, preferred_element_type=jnp.float32),
        "exp",
        scatter_dimension=0,
        tiled=True,
    )
    residual_out = (residual.astype(jnp.float32) + attended).astype(jnp.bfloat16)
    group_rows = routes.shape[0]
    choices_each = routes.shape[1]
    experts = lax.axis_size("exp")
    capacity = 4 * group_rows // experts
    route_flat = routes.reshape(-1)
    expert_ids = lax.broadcasted_iota(jnp.int32, (1, experts), 1)
    onehot = (route_flat[:, None] == expert_ids).astype(jnp.int32)
    slot_index = jnp.sum(jnp.cumsum(onehot, axis=0) * onehot, axis=1) - 1
    target = route_flat * capacity + slot_index
    w_gate = gate_weight[0]
    w_up = up_weight[0]
    hidden_rows = w_gate.shape[0]
    columns = residual_out.shape[1]
    slots = lax.broadcasted_iota(jnp.int32, (experts * capacity, 1), 0)
    placed = target.reshape(group_rows, choices_each)
    picks = jnp.zeros((experts * capacity, group_rows), jnp.bool_)
    for j in range(choices_each):
        picks = picks | (slots == placed[None, :, j])
    buffer = jnp.dot(
        picks.astype(jnp.bfloat16), residual_out, preferred_element_type=jnp.float32
    ).astype(jnp.bfloat16)
    received = lax.all_to_all(
        buffer.reshape(experts, capacity, columns), "exp", split_axis=0, concat_axis=0, tiled=True
    )
    sources, entries, gathered_columns = received.shape
    slices = received.reshape(sources * entries, gathered_columns)
    row_block = lax.all_gather(slices, SEQ, axis=1, tiled=True)
    squares = jnp.einsum("rd,rd->r", slices, slices, preferred_element_type=jnp.float32)
    for axis in reversed(SEQ):
        squares = ring_sum(squares, axis)
    gate_sum = lax.dot_general(w_gate, row_block, contract_last, preferred_element_type=jnp.float32)
    up_sum = lax.dot_general(w_up, row_block, contract_last, preferred_element_type=jnp.float32)
    expert_hidden = finish_rows(gate_sum, up_sum, squares).reshape(hidden_rows, sources, entries)
    return (residual_out, expert_hidden.reshape(1, hidden_rows, experts * capacity))


def solution(mesh):
    torus = Mesh(
        mesh.devices.reshape(4, 4, 2, mesh.shape["exp"]), ("seq_0", "seq_1", "seq_2", "exp")
    )
    in_specs = (
        P(SEQ, "exp"),
        P(SEQ, "exp"),
        P(SEQ, "exp"),
        P(SEQ, "exp"),
        P("exp", SEQ),
        P("exp", SEQ),
        P("exp", None),
        P("exp", SEQ, None),
        P("exp", SEQ, None),
    )
    out_specs = (P("exp", SEQ), P("exp", SEQ, None))
    return jax.shard_map(body, mesh=torus, in_specs=in_specs, out_specs=out_specs, check_vma=False)
```

```python
import jax
import jax.numpy as jnp
from jax import lax
from jax.sharding import Mesh
from jax.sharding import PartitionSpec as P

D = 6144
HEAD_DIM = 128
SEQ = ("seq_0", "seq_1", "seq_2")


precise = lax.Precision.HIGHEST
contract_last = (((1,), (1,)), ((), ()))


def nothing_yet(shard, identity):
    return jax.tree.map(
        lambda a, e: jnp.broadcast_to(jnp.asarray(e, a.dtype), a.shape), shard, identity
    )


def carried_in(shard, axes, combine, identity):
    before = start = nothing_yet(shard, identity)
    so_far = shard
    for axis in reversed(axes):
        peers, place = (lax.axis_size(axis), lax.axis_index(axis))
        pieces = jax.tree.map(lambda part: lax.all_gather(part, axis), so_far)
        inside, so_far = (start, start)
        for k in range(peers):
            passed = k < place
            so_far = combine(so_far, jax.tree.map(lambda part: part[k], pieces))
            inside = jax.tree.map(lambda new, old: jnp.where(passed, new, old), so_far, inside)
        before = combine(inside, before)
    return before


def link_states(earlier, later):
    return (earlier[0] * later[0], later[0][:, None, None] * earlier[1] + later[1])


def send(pair, axis, perm):
    decay, state = pair
    moved = lax.ppermute(state.astype(jnp.bfloat16), axis, perm)
    return (lax.ppermute(decay, axis, perm), moved.astype(jnp.float32))


def swap_cores(pair):
    return jax.tree.map(lambda part: lax.ppermute(part, "seq_2", [(0, 1), (1, 0)]), pair)


def ring_sum(part, axis):
    peers = lax.axis_size(axis)
    total = part
    for d in range(1, peers):
        total = total + lax.ppermute(part, axis, [(i, (i + d) % peers) for i in range(peers)])
    return total


def prefix_over(own, axis):
    peers, place = (lax.axis_size(axis), lax.axis_index(axis))
    shifted = [own] + [
        send(own, axis, [(i, (i + d) % peers) for i in range(peers)]) for d in range(1, peers)
    ]
    start = nothing_yet(own, (1.0, 0.0))
    before, after = (start, start)
    for d in range(1, peers):
        taken = d <= place
        grown = link_states(shifted[d], before)
        before = jax.tree.map(lambda new, old: jnp.where(taken, new, old), grown, before)
    for d in range(peers - 1, 0, -1):
        taken = d > place
        grown = link_states(after, shifted[d])
        after = jax.tree.map(lambda new, old: jnp.where(taken, new, old), grown, after)
    return before, link_states(link_states(before, own), after)


def entering_state(decay, state):
    core = lax.axis_index("seq_2")
    other = swap_cores((decay, state))
    first = jax.tree.map(lambda mine, theirs: jnp.where(core == 0, mine, theirs), (decay, state), other)
    second = jax.tree.map(lambda mine, theirs: jnp.where(core == 0, theirs, mine), (decay, state), other)
    chip = link_states(first, second)
    half = decay.shape[0] // 2
    mine = jax.tree.map(lambda part: lax.dynamic_slice_in_dim(part, core * half, half, 0), chip)
    along_y, row = prefix_over(mine, "seq_1")
    along_x, _ = prefix_over(row, "seq_0")
    chip_before = link_states(along_x, along_y)
    theirs = swap_cores(chip_before)
    whole = jax.tree.map(
        lambda a, b: jnp.where(core == 0, jnp.concatenate([a, b], 0), jnp.concatenate([b, a], 0)),
        chip_before,
        theirs,
    )
    return jnp.where(core == 0, whole[1], first[0][:, None, None] * whole[1] + first[1])


def finish_rows(gate_sum, up_sum, squares):
    inv_rms = lax.rsqrt(squares / D + 1e-06)[None, :]
    return (jax.nn.silu(gate_sum * inv_rms) * (up_sum * inv_rms)).astype(jnp.bfloat16)


def body(
    query_rows,
    key_rows,
    value_rows,
    log_decay,
    out_weight,
    residual,
    routes,
    gate_weight,
    up_weight,
):
    positions, head_cols = query_rows.shape
    heads_here = head_cols // HEAD_DIM
    queries = query_rows.astype(jnp.float32).reshape(positions, heads_here, HEAD_DIM)
    keys_here = key_rows.astype(jnp.float32).reshape(positions, heads_here, HEAD_DIM)
    values_here = value_rows.astype(jnp.float32).reshape(positions, heads_here, HEAD_DIM)
    cumulative = jnp.cumsum(log_decay, axis=0)
    closing = cumulative[-1]
    key_scaled = keys_here * jnp.exp(closing[None, :] - cumulative)[:, :, None]
    local_state = jnp.einsum("shd,she->hde", key_scaled, values_here, precision=precise)
    entering = entering_state(jnp.exp(closing), local_state)
    later = lax.broadcasted_iota(jnp.int32, (positions, positions), 0)
    earlier = lax.broadcasted_iota(jnp.int32, (positions, positions), 1)
    causal = (later >= earlier)[None]
    carried = jnp.einsum(
        "thd,hde->the", queries * jnp.exp(cumulative)[:, :, None], entering, precision=precise
    )
    scores = jnp.einsum("thd,shd->hts", queries, keys_here, precision=precise)
    spread = cumulative.T[:, :, None] - cumulative.T[:, None, :]
    weights = jnp.where(causal, jnp.exp(jnp.where(causal, spread, 0.0)), 0.0)
    within = jnp.einsum("hts,she->the", scores * weights, values_here, precision=precise)
    head_raw = carried + within
    normed = head_raw * lax.rsqrt(jnp.mean(head_raw * head_raw, axis=-1, keepdims=True) + 1e-06)
    normed = normed.astype(jnp.bfloat16).reshape(positions, head_cols)
    gathered = lax.all_gather(normed, SEQ, axis=0, tiled=True)
    row_block = gathered
    attended = lax.psum_scatter(
        lax.dot_general(out_weight, row_block, (((0,), (1,)), ((), ())), preferred_element_type=jnp.float32),
        "exp",
        scatter_dimension=1,
        tiled=True,
    ).T
    residual_out = (residual.astype(jnp.float32) + attended).astype(jnp.bfloat16)
    group_rows = routes.shape[0]
    choices_each = routes.shape[1]
    experts = lax.axis_size("exp")
    capacity = 4 * group_rows // experts
    route_flat = routes.reshape(-1)
    expert_ids = lax.broadcasted_iota(jnp.int32, (1, experts), 1)
    onehot = (route_flat[:, None] == expert_ids).astype(jnp.int32)
    slot_index = jnp.sum(jnp.cumsum(onehot, axis=0) * onehot, axis=1) - 1
    target = route_flat * capacity + slot_index
    w_gate = gate_weight[0]
    w_up = up_weight[0]
    hidden_rows = w_gate.shape[0]
    columns = residual_out.shape[1]
    slots = lax.broadcasted_iota(jnp.int32, (experts * capacity, 1), 0)
    placed = target.reshape(group_rows, choices_each)
    picks = jnp.zeros((experts * capacity, group_rows), jnp.bool_)
    for j in range(choices_each):
        picks = picks | (slots == placed[None, :, j])
    buffer = jnp.dot(
        picks.astype(jnp.bfloat16), residual_out, preferred_element_type=jnp.float32
    ).astype(jnp.bfloat16)
    received = lax.all_to_all(
        buffer.reshape(experts, capacity, columns), "exp", split_axis=0, concat_axis=0, tiled=True
    )
    sources, entries, gathered_columns = received.shape
    slices = received.reshape(sources * entries, gathered_columns)
    row_block = lax.all_gather(slices, SEQ, axis=1, tiled=True)
    squares = jnp.einsum("rd,rd->r", slices, slices, preferred_element_type=jnp.float32)
    for axis in reversed(SEQ):
        squares = ring_sum(squares, axis)
    both = lax.dot_general(
        jnp.concatenate([w_gate, w_up], 0), row_block, contract_last, preferred_element_type=jnp.float32
    )
    gate_sum, up_sum = (both[:hidden_rows], both[hidden_rows:])
    expert_hidden = finish_rows(gate_sum, up_sum, squares).reshape(hidden_rows, sources, entries)
    return (residual_out, expert_hidden.reshape(1, hidden_rows, experts * capacity))


def solution(mesh):
    torus = Mesh(
        mesh.devices.reshape(4, 4, 2, mesh.shape["exp"]), ("seq_0", "seq_1", "seq_2", "exp")
    )
    in_specs = (
        P(SEQ, "exp"),
        P(SEQ, "exp"),
        P(SEQ, "exp"),
        P(SEQ, "exp"),
        P("exp", SEQ),
        P("exp", SEQ),
        P("exp", None),
        P("exp", SEQ, None),
        P("exp", SEQ, None),
    )
    out_specs = (P("exp", SEQ), P("exp", SEQ, None))
    return jax.shard_map(body, mesh=torus, in_specs=in_specs, out_specs=out_specs, check_vma=False)
```

```python
import jax
import jax.numpy as jnp
from jax import lax
from jax.sharding import Mesh
from jax.sharding import PartitionSpec as P

D = 6144
HEAD_DIM = 128
SEQ = ("seq_0", "seq_1", "seq_2")


precise = lax.Precision.HIGHEST
contract_last = (((1,), (1,)), ((), ()))


def nothing_yet(shard, identity):
    return jax.tree.map(
        lambda a, e: jnp.broadcast_to(jnp.asarray(e, a.dtype), a.shape), shard, identity
    )


def carried_in(shard, axes, combine, identity):
    before = start = nothing_yet(shard, identity)
    so_far = shard
    for axis in reversed(axes):
        peers, place = (lax.axis_size(axis), lax.axis_index(axis))
        pieces = jax.tree.map(lambda part: lax.all_gather(part, axis), so_far)
        inside, so_far = (start, start)
        for k in range(peers):
            passed = k < place
            so_far = combine(so_far, jax.tree.map(lambda part: part[k], pieces))
            inside = jax.tree.map(lambda new, old: jnp.where(passed, new, old), so_far, inside)
        before = combine(inside, before)
    return before


def link_states(earlier, later):
    return (earlier[0] * later[0], later[0][:, None, None] * earlier[1] + later[1])


def ring_shifts(part, axis):
    peers = lax.axis_size(axis)
    return [part] + [
        lax.ppermute(part, axis, [(i, (i + d) % peers) for i in range(peers)]) for d in range(1, peers)
    ]


def narrow_shifts(state, axis):
    return [state] + [
        moved.astype(jnp.float32) for moved in ring_shifts(state.astype(jnp.bfloat16), axis)[1:]
    ]


def swap_cores(part):
    return lax.ppermute(part, "seq_2", [(0, 1), (1, 0)])


def ring_sum(part, axis):
    peers = lax.axis_size(axis)
    total = part
    for d in range(1, peers):
        total = total + lax.ppermute(part, axis, [(i, (i + d) % peers) for i in range(peers)])
    return total


def prefix_over(shifted, place):
    peers = len(shifted)
    own = shifted[0]
    start = nothing_yet(own, (1.0, 0.0))
    before, after = (start, start)
    for d in range(1, peers):
        taken = d <= place
        grown = link_states(shifted[d], before)
        before = jax.tree.map(lambda new, old: jnp.where(taken, new, old), grown, before)
    for d in range(peers - 1, 0, -1):
        taken = d > place
        grown = link_states(after, shifted[d])
        after = jax.tree.map(lambda new, old: jnp.where(taken, new, old), grown, after)
    return before, link_states(link_states(before, own), after)


def entering_state(decay, state):
    core = lax.axis_index("seq_2")
    half = decay.shape[0] // 2
    other_decay = swap_cores(decay)
    first_decay = jnp.where(core == 0, decay, other_decay)
    second_decay = jnp.where(core == 0, other_decay, decay)
    mine_decay = lax.dynamic_slice_in_dim(first_decay * second_decay, core * half, half, 0)
    y_decays = ring_shifts(mine_decay, "seq_1")
    row_decay = y_decays[0]
    for part in y_decays[1:]:
        row_decay = row_decay * part
    x_decays = ring_shifts(row_decay, "seq_0")
    other = swap_cores(state)
    first = (first_decay, jnp.where(core == 0, state, other))
    second = (second_decay, jnp.where(core == 0, other, state))
    chip = link_states(first, second)[1]
    mine = lax.dynamic_slice_in_dim(chip, core * half, half, 0)
    y_states = narrow_shifts(mine, "seq_1")
    along_y, row = prefix_over(list(zip(y_decays, y_states)), lax.axis_index("seq_1"))
    x_states = narrow_shifts(row[1], "seq_0")
    along_x, _ = prefix_over(list(zip(x_decays, x_states)), lax.axis_index("seq_0"))
    chip_before = link_states(along_x, along_y)[1]
    theirs = swap_cores(chip_before)
    whole = jnp.where(
        core == 0, jnp.concatenate([chip_before, theirs], 0), jnp.concatenate([theirs, chip_before], 0)
    )
    return jnp.where(core == 0, whole, first[0][:, None, None] * whole + first[1])


def finish_rows(gate_sum, up_sum, squares):
    inv_rms = lax.rsqrt(squares / D + 1e-06)[None, :]
    return (jax.nn.silu(gate_sum * inv_rms) * (up_sum * inv_rms)).astype(jnp.bfloat16)


def body(
    query_rows,
    key_rows,
    value_rows,
    log_decay,
    out_weight,
    residual,
    routes,
    gate_weight,
    up_weight,
):
    positions, head_cols = query_rows.shape
    heads_here = head_cols // HEAD_DIM
    queries = query_rows.astype(jnp.float32).reshape(positions, heads_here, HEAD_DIM)
    keys_here = key_rows.astype(jnp.float32).reshape(positions, heads_here, HEAD_DIM)
    values_here = value_rows.astype(jnp.float32).reshape(positions, heads_here, HEAD_DIM)
    cumulative = jnp.cumsum(log_decay, axis=0)
    closing = cumulative[-1]
    key_scaled = keys_here * jnp.exp(closing[None, :] - cumulative)[:, :, None]
    local_state = jnp.einsum("shd,she->hde", key_scaled, values_here, precision=precise)
    entering = entering_state(jnp.exp(closing), local_state)
    later = lax.broadcasted_iota(jnp.int32, (positions, positions), 0)
    earlier = lax.broadcasted_iota(jnp.int32, (positions, positions), 1)
    causal = (later >= earlier)[None]
    carried = jnp.einsum(
        "thd,hde->the", queries * jnp.exp(cumulative)[:, :, None], entering, precision=precise
    )
    scores = jnp.einsum("thd,shd->hts", queries, keys_here, precision=precise)
    spread = cumulative.T[:, :, None] - cumulative.T[:, None, :]
    weights = jnp.where(causal, jnp.exp(jnp.where(causal, spread, 0.0)), 0.0)
    within = jnp.einsum("hts,she->the", scores * weights, values_here, precision=precise)
    head_raw = carried + within
    normed = head_raw * lax.rsqrt(jnp.mean(head_raw * head_raw, axis=-1, keepdims=True) + 1e-06)
    normed = normed.astype(jnp.bfloat16).reshape(positions, head_cols)
    gathered = lax.all_gather(normed, SEQ, axis=0, tiled=True)
    row_block = gathered
    attended = lax.psum_scatter(
        lax.dot_general(out_weight, row_block, (((0,), (1,)), ((), ())), preferred_element_type=jnp.float32),
        "exp",
        scatter_dimension=1,
        tiled=True,
    ).T
    residual_out = (residual.astype(jnp.float32) + attended).astype(jnp.bfloat16)
    group_rows = routes.shape[0]
    choices_each = routes.shape[1]
    experts = lax.axis_size("exp")
    capacity = 4 * group_rows // experts
    route_flat = routes.reshape(-1)
    expert_ids = lax.broadcasted_iota(jnp.int32, (1, experts), 1)
    onehot = (route_flat[:, None] == expert_ids).astype(jnp.int32)
    slot_index = jnp.sum(jnp.cumsum(onehot, axis=0) * onehot, axis=1) - 1
    target = route_flat * capacity + slot_index
    w_gate = gate_weight[0]
    w_up = up_weight[0]
    hidden_rows = w_gate.shape[0]
    columns = residual_out.shape[1]
    slots = lax.broadcasted_iota(jnp.int32, (experts * capacity, 1), 0)
    placed = target.reshape(group_rows, choices_each)
    picks = jnp.zeros((experts * capacity, group_rows), jnp.bool_)
    for j in range(choices_each):
        picks = picks | (slots == placed[None, :, j])
    buffer = jnp.dot(
        picks.astype(jnp.bfloat16), residual_out, preferred_element_type=jnp.float32
    ).astype(jnp.bfloat16)
    received = lax.all_to_all(
        buffer.reshape(experts, capacity, columns), "exp", split_axis=0, concat_axis=0, tiled=True
    )
    sources, entries, gathered_columns = received.shape
    slices = received.reshape(sources * entries, gathered_columns)
    row_block = lax.all_gather(slices, SEQ, axis=1, tiled=True)
    squares = jnp.einsum("rd,rd->r", slices, slices, preferred_element_type=jnp.float32)
    for axis in reversed(SEQ):
        squares = ring_sum(squares, axis)
    both = lax.dot_general(
        jnp.concatenate([w_gate, w_up], 0), row_block, contract_last, preferred_element_type=jnp.float32
    )
    gate_sum, up_sum = (both[:hidden_rows], both[hidden_rows:])
    expert_hidden = finish_rows(gate_sum, up_sum, squares).reshape(hidden_rows, sources, entries)
    return (residual_out, expert_hidden.reshape(1, hidden_rows, experts * capacity))


def solution(mesh):
    torus = Mesh(
        mesh.devices.reshape(4, 4, 2, mesh.shape["exp"]), ("seq_0", "seq_1", "seq_2", "exp")
    )
    in_specs = (
        P(SEQ, "exp"),
        P(SEQ, "exp"),
        P(SEQ, "exp"),
        P(SEQ, "exp"),
        P("exp", SEQ),
        P("exp", SEQ),
        P("exp", None),
        P("exp", SEQ, None),
        P("exp", SEQ, None),
    )
    out_specs = (P("exp", SEQ), P("exp", SEQ, None))
    return jax.shard_map(body, mesh=torus, in_specs=in_specs, out_specs=out_specs, check_vma=False)
```

```python
import jax
import jax.numpy as jnp
from jax import lax
from jax.sharding import Mesh
from jax.sharding import PartitionSpec as P

D = 6144
HEAD_DIM = 128
SEQ = ("seq_0", "seq_1", "seq_2")


precise = lax.Precision.HIGHEST
contract_last = (((1,), (1,)), ((), ()))


def nothing_yet(shard, identity):
    return jax.tree.map(
        lambda a, e: jnp.broadcast_to(jnp.asarray(e, a.dtype), a.shape), shard, identity
    )


def carried_in(shard, axes, combine, identity):
    before = start = nothing_yet(shard, identity)
    so_far = shard
    for axis in reversed(axes):
        peers, place = (lax.axis_size(axis), lax.axis_index(axis))
        pieces = jax.tree.map(lambda part: lax.all_gather(part, axis), so_far)
        inside, so_far = (start, start)
        for k in range(peers):
            passed = k < place
            so_far = combine(so_far, jax.tree.map(lambda part: part[k], pieces))
            inside = jax.tree.map(lambda new, old: jnp.where(passed, new, old), so_far, inside)
        before = combine(inside, before)
    return before


def link_states(earlier, later):
    return (earlier[0] * later[0], later[0][:, None, None] * earlier[1] + later[1])


def ring_shifts(part, axis):
    peers = lax.axis_size(axis)
    return [part] + [
        lax.ppermute(part, axis, [(i, (i + d) % peers) for i in range(peers)]) for d in range(1, peers)
    ]


def packed_shifts(decay, state, axis):
    heads, rows, cols = state.shape
    high = decay.astype(jnp.bfloat16)
    low = (decay - high.astype(jnp.float32)).astype(jnp.bfloat16)
    tail = jnp.concatenate(
        [
            jnp.broadcast_to(high[:, None, None], (heads, 1, cols)),
            jnp.broadcast_to(low[:, None, None], (heads, 1, cols)),
            jnp.zeros((heads, 6, cols), jnp.bfloat16),
        ],
        axis=1,
    )
    packed = jnp.concatenate([state.astype(jnp.bfloat16), tail], axis=1)
    pieces = [(decay, state)]
    for moved in ring_shifts(packed, axis)[1:]:
        whole = moved.astype(jnp.float32)
        pieces.append((whole[:, rows, 0] + whole[:, rows + 1, 0], whole[:, :rows]))
    return pieces


def swap_cores(part):
    return lax.ppermute(part, "seq_2", [(0, 1), (1, 0)])


def ring_sum(part, axis):
    peers = lax.axis_size(axis)
    total = part
    for d in range(1, peers):
        total = total + lax.ppermute(part, axis, [(i, (i + d) % peers) for i in range(peers)])
    return total


def prefix_over(shifted, place):
    peers = len(shifted)
    own = shifted[0]
    start = nothing_yet(own, (1.0, 0.0))
    before, after = (start, start)
    for d in range(1, peers):
        taken = d <= place
        grown = link_states(shifted[d], before)
        before = jax.tree.map(lambda new, old: jnp.where(taken, new, old), grown, before)
    for d in range(peers - 1, 0, -1):
        taken = d > place
        grown = link_states(after, shifted[d])
        after = jax.tree.map(lambda new, old: jnp.where(taken, new, old), grown, after)
    return before, link_states(link_states(before, own), after)


def entering_state(decay, state):
    core = lax.axis_index("seq_2")
    half = decay.shape[0] // 2
    other = (swap_cores(decay), swap_cores(state))
    first = jax.tree.map(lambda mine, theirs: jnp.where(core == 0, mine, theirs), (decay, state), other)
    second = jax.tree.map(lambda mine, theirs: jnp.where(core == 0, theirs, mine), (decay, state), other)
    chip = link_states(first, second)
    mine = jax.tree.map(lambda part: lax.dynamic_slice_in_dim(part, core * half, half, 0), chip)
    along_y, row = prefix_over(packed_shifts(*mine, "seq_1"), lax.axis_index("seq_1"))
    along_x, _ = prefix_over(packed_shifts(*row, "seq_0"), lax.axis_index("seq_0"))
    chip_before = link_states(along_x, along_y)[1]
    theirs = swap_cores(chip_before)
    whole = jnp.where(
        core == 0, jnp.concatenate([chip_before, theirs], 0), jnp.concatenate([theirs, chip_before], 0)
    )
    return jnp.where(core == 0, whole, first[0][:, None, None] * whole + first[1])


def finish_rows(gate_sum, up_sum, squares):
    inv_rms = lax.rsqrt(squares / D + 1e-06)[None, :]
    return (jax.nn.silu(gate_sum * inv_rms) * (up_sum * inv_rms)).astype(jnp.bfloat16)


def body(
    query_rows,
    key_rows,
    value_rows,
    log_decay,
    out_weight,
    residual,
    routes,
    gate_weight,
    up_weight,
):
    positions, head_cols = query_rows.shape
    heads_here = head_cols // HEAD_DIM
    queries = query_rows.astype(jnp.float32).reshape(positions, heads_here, HEAD_DIM)
    keys_here = key_rows.astype(jnp.float32).reshape(positions, heads_here, HEAD_DIM)
    values_here = value_rows.astype(jnp.float32).reshape(positions, heads_here, HEAD_DIM)
    cumulative = jnp.cumsum(log_decay, axis=0)
    closing = cumulative[-1]
    key_scaled = keys_here * jnp.exp(closing[None, :] - cumulative)[:, :, None]
    local_state = jnp.einsum("shd,she->hde", key_scaled, values_here, precision=precise)
    entering = entering_state(jnp.exp(closing), local_state)
    later = lax.broadcasted_iota(jnp.int32, (positions, positions), 0)
    earlier = lax.broadcasted_iota(jnp.int32, (positions, positions), 1)
    causal = (later >= earlier)[None]
    carried = jnp.einsum(
        "thd,hde->the", queries * jnp.exp(cumulative)[:, :, None], entering, precision=precise
    )
    scores = jnp.einsum("thd,shd->hts", queries, keys_here, precision=precise)
    spread = cumulative.T[:, :, None] - cumulative.T[:, None, :]
    weights = jnp.where(causal, jnp.exp(jnp.where(causal, spread, 0.0)), 0.0)
    within = jnp.einsum("hts,she->the", scores * weights, values_here, precision=precise)
    head_raw = carried + within
    normed = head_raw * lax.rsqrt(jnp.mean(head_raw * head_raw, axis=-1, keepdims=True) + 1e-06)
    normed = normed.astype(jnp.bfloat16).reshape(positions, head_cols)
    gathered = lax.all_gather(normed, SEQ, axis=0, tiled=True)
    row_block = gathered
    attended = lax.psum_scatter(
        lax.dot_general(out_weight, row_block, (((0,), (1,)), ((), ())), preferred_element_type=jnp.float32),
        "exp",
        scatter_dimension=1,
        tiled=True,
    ).T
    residual_out = (residual.astype(jnp.float32) + attended).astype(jnp.bfloat16)
    group_rows = routes.shape[0]
    choices_each = routes.shape[1]
    experts = lax.axis_size("exp")
    capacity = 4 * group_rows // experts
    route_flat = routes.reshape(-1)
    expert_ids = lax.broadcasted_iota(jnp.int32, (1, experts), 1)
    onehot = (route_flat[:, None] == expert_ids).astype(jnp.int32)
    slot_index = jnp.sum(jnp.cumsum(onehot, axis=0) * onehot, axis=1) - 1
    target = route_flat * capacity + slot_index
    w_gate = gate_weight[0]
    w_up = up_weight[0]
    hidden_rows = w_gate.shape[0]
    columns = residual_out.shape[1]
    slots = lax.broadcasted_iota(jnp.int32, (experts * capacity, 1), 0)
    placed = target.reshape(group_rows, choices_each)
    picks = jnp.zeros((experts * capacity, group_rows), jnp.bool_)
    for j in range(choices_each):
        picks = picks | (slots == placed[None, :, j])
    buffer = jnp.dot(
        picks.astype(jnp.bfloat16), residual_out, preferred_element_type=jnp.float32
    ).astype(jnp.bfloat16)
    received = lax.all_to_all(
        buffer.reshape(experts, capacity, columns), "exp", split_axis=0, concat_axis=0, tiled=True
    )
    sources, entries, gathered_columns = received.shape
    slices = received.reshape(sources * entries, gathered_columns)
    row_block = lax.all_gather(slices, SEQ, axis=1, tiled=True)
    squares = jnp.einsum("rd,rd->r", slices, slices, preferred_element_type=jnp.float32)
    for axis in reversed(SEQ):
        squares = ring_sum(squares, axis)
    both = lax.dot_general(
        jnp.concatenate([w_gate, w_up], 0), row_block, contract_last, preferred_element_type=jnp.float32
    )
    gate_sum, up_sum = (both[:hidden_rows], both[hidden_rows:])
    expert_hidden = finish_rows(gate_sum, up_sum, squares).reshape(hidden_rows, sources, entries)
    return (residual_out, expert_hidden.reshape(1, hidden_rows, experts * capacity))


def solution(mesh):
    torus = Mesh(
        mesh.devices.reshape(4, 4, 2, mesh.shape["exp"]), ("seq_0", "seq_1", "seq_2", "exp")
    )
    in_specs = (
        P(SEQ, "exp"),
        P(SEQ, "exp"),
        P(SEQ, "exp"),
        P(SEQ, "exp"),
        P("exp", SEQ),
        P("exp", SEQ),
        P("exp", None),
        P("exp", SEQ, None),
        P("exp", SEQ, None),
    )
    out_specs = (P("exp", SEQ), P("exp", SEQ, None))
    return jax.shard_map(body, mesh=torus, in_specs=in_specs, out_specs=out_specs, check_vma=False)
```

```python
import jax
import jax.numpy as jnp
from jax import lax
from jax.sharding import Mesh
from jax.sharding import PartitionSpec as P

D = 6144
HEAD_DIM = 128
SEQ = ("seq_0", "seq_1", "seq_2")


precise = lax.Precision.HIGHEST
contract_last = (((1,), (1,)), ((), ()))


def nothing_yet(shard, identity):
    return jax.tree.map(
        lambda a, e: jnp.broadcast_to(jnp.asarray(e, a.dtype), a.shape), shard, identity
    )


def carried_in(shard, axes, combine, identity):
    before = start = nothing_yet(shard, identity)
    so_far = shard
    for axis in reversed(axes):
        peers, place = (lax.axis_size(axis), lax.axis_index(axis))
        pieces = jax.tree.map(lambda part: lax.all_gather(part, axis), so_far)
        inside, so_far = (start, start)
        for k in range(peers):
            passed = k < place
            so_far = combine(so_far, jax.tree.map(lambda part: part[k], pieces))
            inside = jax.tree.map(lambda new, old: jnp.where(passed, new, old), so_far, inside)
        before = combine(inside, before)
    return before


def link_states(earlier, later):
    return (earlier[0] * later[0], later[0][:, None, None] * earlier[1] + later[1])


def ring_shifts(part, axis):
    peers = lax.axis_size(axis)
    return [part] + [
        lax.ppermute(part, axis, [(i, (i + d) % peers) for i in range(peers)]) for d in range(1, peers)
    ]


def packed_shifts(decay, state, axis):
    heads, rows, cols = state.shape
    scaled = decay * 65537.0
    leading = scaled - (scaled - decay)
    high = leading.astype(jnp.bfloat16)
    low = (decay - leading).astype(jnp.bfloat16)
    tail = jnp.concatenate(
        [
            jnp.broadcast_to(high[:, None, None], (heads, 1, cols)),
            jnp.broadcast_to(low[:, None, None], (heads, 1, cols)),
            jnp.zeros((heads, 6, cols), jnp.bfloat16),
        ],
        axis=1,
    )
    packed = jnp.concatenate([state.astype(jnp.bfloat16), tail], axis=1)
    pieces = [(decay, state)]
    for moved in ring_shifts(packed, axis)[1:]:
        whole = moved.astype(jnp.float32)
        pieces.append((whole[:, rows, 0] + whole[:, rows + 1, 0], whole[:, :rows]))
    return pieces


def swap_cores(part):
    return lax.ppermute(part, "seq_2", [(0, 1), (1, 0)])


def ring_sum(part, axis):
    peers = lax.axis_size(axis)
    total = part
    for d in range(1, peers):
        total = total + lax.ppermute(part, axis, [(i, (i + d) % peers) for i in range(peers)])
    return total


def prefix_over(shifted, place):
    peers = len(shifted)
    own = shifted[0]
    start = nothing_yet(own, (1.0, 0.0))
    before, after = (start, start)
    for d in range(1, peers):
        taken = d <= place
        grown = link_states(shifted[d], before)
        before = jax.tree.map(lambda new, old: jnp.where(taken, new, old), grown, before)
    for d in range(peers - 1, 0, -1):
        taken = d > place
        grown = link_states(after, shifted[d])
        after = jax.tree.map(lambda new, old: jnp.where(taken, new, old), grown, after)
    return before, link_states(link_states(before, own), after)


def entering_state(decay, state):
    core = lax.axis_index("seq_2")
    half = decay.shape[0] // 2
    other = (swap_cores(decay), swap_cores(state))
    first = jax.tree.map(lambda mine, theirs: jnp.where(core == 0, mine, theirs), (decay, state), other)
    second = jax.tree.map(lambda mine, theirs: jnp.where(core == 0, theirs, mine), (decay, state), other)
    chip = link_states(first, second)
    mine = jax.tree.map(lambda part: lax.dynamic_slice_in_dim(part, core * half, half, 0), chip)
    along_y, row = prefix_over(packed_shifts(*mine, "seq_1"), lax.axis_index("seq_1"))
    along_x, _ = prefix_over(packed_shifts(*row, "seq_0"), lax.axis_index("seq_0"))
    chip_before = link_states(along_x, along_y)[1]
    theirs = swap_cores(chip_before)
    whole = jnp.where(
        core == 0, jnp.concatenate([chip_before, theirs], 0), jnp.concatenate([theirs, chip_before], 0)
    )
    return jnp.where(core == 0, whole, first[0][:, None, None] * whole + first[1])


def finish_rows(gate_sum, up_sum, squares):
    inv_rms = lax.rsqrt(squares / D + 1e-06)[None, :]
    return (jax.nn.silu(gate_sum * inv_rms) * (up_sum * inv_rms)).astype(jnp.bfloat16)


def body(
    query_rows,
    key_rows,
    value_rows,
    log_decay,
    out_weight,
    residual,
    routes,
    gate_weight,
    up_weight,
):
    positions, head_cols = query_rows.shape
    heads_here = head_cols // HEAD_DIM
    queries = query_rows.astype(jnp.float32).reshape(positions, heads_here, HEAD_DIM)
    keys_here = key_rows.astype(jnp.float32).reshape(positions, heads_here, HEAD_DIM)
    values_here = value_rows.astype(jnp.float32).reshape(positions, heads_here, HEAD_DIM)
    cumulative = jnp.cumsum(log_decay, axis=0)
    closing = cumulative[-1]
    key_scaled = keys_here * jnp.exp(closing[None, :] - cumulative)[:, :, None]
    local_state = jnp.einsum("shd,she->hde", key_scaled, values_here, precision=precise)
    entering = entering_state(jnp.exp(closing), local_state)
    later = lax.broadcasted_iota(jnp.int32, (positions, positions), 0)
    earlier = lax.broadcasted_iota(jnp.int32, (positions, positions), 1)
    causal = (later >= earlier)[None]
    carried = jnp.einsum(
        "thd,hde->the", queries * jnp.exp(cumulative)[:, :, None], entering, precision=precise
    )
    scores = jnp.einsum("thd,shd->hts", queries, keys_here, precision=precise)
    spread = cumulative.T[:, :, None] - cumulative.T[:, None, :]
    weights = jnp.where(causal, jnp.exp(jnp.where(causal, spread, 0.0)), 0.0)
    within = jnp.einsum("hts,she->the", scores * weights, values_here, precision=precise)
    head_raw = carried + within
    normed = head_raw * lax.rsqrt(jnp.mean(head_raw * head_raw, axis=-1, keepdims=True) + 1e-06)
    normed = normed.astype(jnp.bfloat16).reshape(positions, head_cols)
    gathered = lax.all_gather(normed, SEQ, axis=0, tiled=True)
    row_block = gathered
    attended = lax.psum_scatter(
        lax.dot_general(out_weight, row_block, (((0,), (1,)), ((), ())), preferred_element_type=jnp.float32),
        "exp",
        scatter_dimension=1,
        tiled=True,
    ).T
    residual_out = (residual.astype(jnp.float32) + attended).astype(jnp.bfloat16)
    group_rows = routes.shape[0]
    choices_each = routes.shape[1]
    experts = lax.axis_size("exp")
    capacity = 4 * group_rows // experts
    route_flat = routes.reshape(-1)
    expert_ids = lax.broadcasted_iota(jnp.int32, (1, experts), 1)
    onehot = (route_flat[:, None] == expert_ids).astype(jnp.int32)
    slot_index = jnp.sum(jnp.cumsum(onehot, axis=0) * onehot, axis=1) - 1
    target = route_flat * capacity + slot_index
    w_gate = gate_weight[0]
    w_up = up_weight[0]
    hidden_rows = w_gate.shape[0]
    columns = residual_out.shape[1]
    slots = lax.broadcasted_iota(jnp.int32, (experts * capacity, 1), 0)
    placed = target.reshape(group_rows, choices_each)
    picks = jnp.zeros((experts * capacity, group_rows), jnp.bool_)
    for j in range(choices_each):
        picks = picks | (slots == placed[None, :, j])
    buffer = jnp.dot(
        picks.astype(jnp.bfloat16), residual_out, preferred_element_type=jnp.float32
    ).astype(jnp.bfloat16)
    received = lax.all_to_all(
        buffer.reshape(experts, capacity, columns), "exp", split_axis=0, concat_axis=0, tiled=True
    )
    sources, entries, gathered_columns = received.shape
    slices = received.reshape(sources * entries, gathered_columns)
    row_block = lax.all_gather(slices, SEQ, axis=1, tiled=True)
    squares = jnp.einsum("rd,rd->r", slices, slices, preferred_element_type=jnp.float32)
    for axis in reversed(SEQ):
        squares = ring_sum(squares, axis)
    both = lax.dot_general(
        jnp.concatenate([w_gate, w_up], 0), row_block, contract_last, preferred_element_type=jnp.float32
    )
    gate_sum, up_sum = (both[:hidden_rows], both[hidden_rows:])
    expert_hidden = finish_rows(gate_sum, up_sum, squares).reshape(hidden_rows, sources, entries)
    return (residual_out, expert_hidden.reshape(1, hidden_rows, experts * capacity))


def solution(mesh):
    torus = Mesh(
        mesh.devices.reshape(4, 4, 2, mesh.shape["exp"]), ("seq_0", "seq_1", "seq_2", "exp")
    )
    in_specs = (
        P(SEQ, "exp"),
        P(SEQ, "exp"),
        P(SEQ, "exp"),
        P(SEQ, "exp"),
        P("exp", SEQ),
        P("exp", SEQ),
        P("exp", None),
        P("exp", SEQ, None),
        P("exp", SEQ, None),
    )
    out_specs = (P("exp", SEQ), P("exp", SEQ, None))
    return jax.shard_map(body, mesh=torus, in_specs=in_specs, out_specs=out_specs, check_vma=False)
```

```python
import jax
import jax.numpy as jnp
from jax import lax
from jax.sharding import Mesh
from jax.sharding import PartitionSpec as P

D = 6144
HEAD_DIM = 128
SEQ = ("seq_0", "seq_1", "seq_2")


precise = lax.Precision.HIGHEST
contract_last = (((1,), (1,)), ((), ()))


def nothing_yet(shard, identity):
    return jax.tree.map(
        lambda a, e: jnp.broadcast_to(jnp.asarray(e, a.dtype), a.shape), shard, identity
    )


def carried_in(shard, axes, combine, identity):
    before = start = nothing_yet(shard, identity)
    so_far = shard
    for axis in reversed(axes):
        peers, place = (lax.axis_size(axis), lax.axis_index(axis))
        pieces = jax.tree.map(lambda part: lax.all_gather(part, axis), so_far)
        inside, so_far = (start, start)
        for k in range(peers):
            passed = k < place
            so_far = combine(so_far, jax.tree.map(lambda part: part[k], pieces))
            inside = jax.tree.map(lambda new, old: jnp.where(passed, new, old), so_far, inside)
        before = combine(inside, before)
    return before


def link_states(earlier, later):
    return (earlier[0] * later[0], later[0][:, None, None] * earlier[1] + later[1])


def ring_shifts(part, axis, wrap=True):
    peers = lax.axis_size(axis)
    return [part] + [
        lax.ppermute(part, axis, [(i, (i + d) % peers) for i in range(peers if wrap else peers - d)])
        for d in range(1, peers)
    ]


def packed_shifts(decay, state, axis, wrap=True):
    heads, rows, cols = state.shape
    scaled = decay * 65537.0
    leading = scaled - (scaled - decay)
    high = leading.astype(jnp.bfloat16)
    low = (decay - leading).astype(jnp.bfloat16)
    tail = jnp.concatenate(
        [
            jnp.broadcast_to(high[:, None, None], (heads, 1, cols)),
            jnp.broadcast_to(low[:, None, None], (heads, 1, cols)),
            jnp.zeros((heads, 6, cols), jnp.bfloat16),
        ],
        axis=1,
    )
    packed = jnp.concatenate([state.astype(jnp.bfloat16), tail], axis=1)
    pieces = [(decay, state)]
    for moved in ring_shifts(packed, axis, wrap)[1:]:
        whole = moved.astype(jnp.float32)
        pieces.append((whole[:, rows, 0] + whole[:, rows + 1, 0], whole[:, :rows]))
    return pieces


def swap_cores(part):
    return lax.ppermute(part, "seq_2", [(0, 1), (1, 0)])


def ring_sum(part, axis):
    peers = lax.axis_size(axis)
    total = part
    for d in range(1, peers):
        total = total + lax.ppermute(part, axis, [(i, (i + d) % peers) for i in range(peers)])
    return total


def prefix_over(shifted, place):
    peers = len(shifted)
    own = shifted[0]
    start = nothing_yet(own, (1.0, 0.0))
    before, after = (start, start)
    for d in range(1, peers):
        taken = d <= place
        grown = link_states(shifted[d], before)
        before = jax.tree.map(lambda new, old: jnp.where(taken, new, old), grown, before)
    for d in range(peers - 1, 0, -1):
        taken = d > place
        grown = link_states(after, shifted[d])
        after = jax.tree.map(lambda new, old: jnp.where(taken, new, old), grown, after)
    return before, link_states(link_states(before, own), after)


def entering_state(decay, state):
    core = lax.axis_index("seq_2")
    half = decay.shape[0] // 2
    other = (swap_cores(decay), swap_cores(state))
    first = jax.tree.map(lambda mine, theirs: jnp.where(core == 0, mine, theirs), (decay, state), other)
    second = jax.tree.map(lambda mine, theirs: jnp.where(core == 0, theirs, mine), (decay, state), other)
    chip = link_states(first, second)
    mine = jax.tree.map(lambda part: lax.dynamic_slice_in_dim(part, core * half, half, 0), chip)
    along_y, row = prefix_over(packed_shifts(*mine, "seq_1"), lax.axis_index("seq_1"))
    along_x, _ = prefix_over(packed_shifts(*row, "seq_0", wrap=False), lax.axis_index("seq_0"))
    chip_before = link_states(along_x, along_y)[1]
    theirs = swap_cores(chip_before)
    whole = jnp.where(
        core == 0, jnp.concatenate([chip_before, theirs], 0), jnp.concatenate([theirs, chip_before], 0)
    )
    return jnp.where(core == 0, whole, first[0][:, None, None] * whole + first[1])


def finish_rows(gate_sum, up_sum, squares):
    inv_rms = lax.rsqrt(squares / D + 1e-06)[None, :]
    return (jax.nn.silu(gate_sum * inv_rms) * (up_sum * inv_rms)).astype(jnp.bfloat16)


def body(
    query_rows,
    key_rows,
    value_rows,
    log_decay,
    out_weight,
    residual,
    routes,
    gate_weight,
    up_weight,
):
    positions, head_cols = query_rows.shape
    heads_here = head_cols // HEAD_DIM
    queries = query_rows.astype(jnp.float32).reshape(positions, heads_here, HEAD_DIM)
    keys_here = key_rows.astype(jnp.float32).reshape(positions, heads_here, HEAD_DIM)
    values_here = value_rows.astype(jnp.float32).reshape(positions, heads_here, HEAD_DIM)
    cumulative = jnp.cumsum(log_decay, axis=0)
    closing = cumulative[-1]
    key_scaled = keys_here * jnp.exp(closing[None, :] - cumulative)[:, :, None]
    local_state = jnp.einsum("shd,she->hde", key_scaled, values_here, precision=precise)
    entering = entering_state(jnp.exp(closing), local_state)
    later = lax.broadcasted_iota(jnp.int32, (positions, positions), 0)
    earlier = lax.broadcasted_iota(jnp.int32, (positions, positions), 1)
    causal = (later >= earlier)[None]
    carried = jnp.einsum(
        "thd,hde->the", queries * jnp.exp(cumulative)[:, :, None], entering, precision=precise
    )
    scores = jnp.einsum("thd,shd->hts", queries, keys_here, precision=precise)
    spread = cumulative.T[:, :, None] - cumulative.T[:, None, :]
    weights = jnp.where(causal, jnp.exp(jnp.where(causal, spread, 0.0)), 0.0)
    within = jnp.einsum("hts,she->the", scores * weights, values_here, precision=precise)
    head_raw = carried + within
    normed = head_raw * lax.rsqrt(jnp.mean(head_raw * head_raw, axis=-1, keepdims=True) + 1e-06)
    normed = normed.astype(jnp.bfloat16).reshape(positions, head_cols)
    gathered = lax.all_gather(normed, SEQ, axis=0, tiled=True)
    row_block = gathered
    attended = lax.psum_scatter(
        lax.dot_general(out_weight, row_block, (((0,), (1,)), ((), ())), preferred_element_type=jnp.float32),
        "exp",
        scatter_dimension=1,
        tiled=True,
    ).T
    residual_out = (residual.astype(jnp.float32) + attended).astype(jnp.bfloat16)
    group_rows = routes.shape[0]
    choices_each = routes.shape[1]
    experts = lax.axis_size("exp")
    capacity = 4 * group_rows // experts
    route_flat = routes.reshape(-1)
    expert_ids = lax.broadcasted_iota(jnp.int32, (1, experts), 1)
    onehot = (route_flat[:, None] == expert_ids).astype(jnp.int32)
    slot_index = jnp.sum(jnp.cumsum(onehot, axis=0) * onehot, axis=1) - 1
    target = route_flat * capacity + slot_index
    w_gate = gate_weight[0]
    w_up = up_weight[0]
    hidden_rows = w_gate.shape[0]
    columns = residual_out.shape[1]
    slots = lax.broadcasted_iota(jnp.int32, (experts * capacity, 1), 0)
    placed = target.reshape(group_rows, choices_each)
    picks = jnp.zeros((experts * capacity, group_rows), jnp.bool_)
    for j in range(choices_each):
        picks = picks | (slots == placed[None, :, j])
    buffer = jnp.dot(
        picks.astype(jnp.bfloat16), residual_out, preferred_element_type=jnp.float32
    ).astype(jnp.bfloat16)
    received = lax.all_to_all(
        buffer.reshape(experts, capacity, columns), "exp", split_axis=0, concat_axis=0, tiled=True
    )
    sources, entries, gathered_columns = received.shape
    slices = received.reshape(sources * entries, gathered_columns)
    row_block = lax.all_gather(slices, SEQ, axis=1, tiled=True)
    squares = jnp.einsum("rd,rd->r", slices, slices, preferred_element_type=jnp.float32)
    for axis in reversed(SEQ):
        squares = ring_sum(squares, axis)
    both = lax.dot_general(
        jnp.concatenate([w_gate, w_up], 0), row_block, contract_last, preferred_element_type=jnp.float32
    )
    gate_sum, up_sum = (both[:hidden_rows], both[hidden_rows:])
    expert_hidden = finish_rows(gate_sum, up_sum, squares).reshape(hidden_rows, sources, entries)
    return (residual_out, expert_hidden.reshape(1, hidden_rows, experts * capacity))


def solution(mesh):
    torus = Mesh(
        mesh.devices.reshape(4, 4, 2, mesh.shape["exp"]), ("seq_0", "seq_1", "seq_2", "exp")
    )
    in_specs = (
        P(SEQ, "exp"),
        P(SEQ, "exp"),
        P(SEQ, "exp"),
        P(SEQ, "exp"),
        P("exp", SEQ),
        P("exp", SEQ),
        P("exp", None),
        P("exp", SEQ, None),
        P("exp", SEQ, None),
    )
    out_specs = (P("exp", SEQ), P("exp", SEQ, None))
    return jax.shard_map(body, mesh=torus, in_specs=in_specs, out_specs=out_specs, check_vma=False)
```

```python
import jax
import jax.numpy as jnp
from jax import lax
from jax.sharding import Mesh
from jax.sharding import PartitionSpec as P

D = 6144
HEAD_DIM = 128
SEQ = ("seq_0", "seq_1", "seq_2")


precise = lax.Precision.HIGHEST
contract_last = (((1,), (1,)), ((), ()))


def nothing_yet(shard, identity):
    return jax.tree.map(
        lambda a, e: jnp.broadcast_to(jnp.asarray(e, a.dtype), a.shape), shard, identity
    )


def carried_in(shard, axes, combine, identity):
    before = start = nothing_yet(shard, identity)
    so_far = shard
    for axis in reversed(axes):
        peers, place = (lax.axis_size(axis), lax.axis_index(axis))
        pieces = jax.tree.map(lambda part: lax.all_gather(part, axis), so_far)
        inside, so_far = (start, start)
        for k in range(peers):
            passed = k < place
            so_far = combine(so_far, jax.tree.map(lambda part: part[k], pieces))
            inside = jax.tree.map(lambda new, old: jnp.where(passed, new, old), so_far, inside)
        before = combine(inside, before)
    return before


def link_states(earlier, later):
    return (earlier[0] * later[0], later[0][:, None, None] * earlier[1] + later[1])


def ring_shifts(part, axis):
    peers = lax.axis_size(axis)
    return [part] + [
        lax.ppermute(part, axis, [(i, (i + d) % peers) for i in range(peers)]) for d in range(1, peers)
    ]


def packed_shifts(decay, state, axis):
    heads, rows, cols = state.shape
    scaled = decay * 65537.0
    leading = scaled - (scaled - decay)
    high = leading.astype(jnp.bfloat16)
    low = (decay - leading).astype(jnp.bfloat16)
    tail = jnp.concatenate(
        [
            jnp.broadcast_to(high[:, None, None], (heads, 1, cols)),
            jnp.broadcast_to(low[:, None, None], (heads, 1, cols)),
            jnp.zeros((heads, 6, cols), jnp.bfloat16),
        ],
        axis=1,
    )
    packed = jnp.concatenate([state.astype(jnp.bfloat16), tail], axis=1)
    pieces = [(decay, state)]
    for moved in ring_shifts(packed, axis)[1:]:
        whole = moved.astype(jnp.float32)
        pieces.append((whole[:, rows, 0] + whole[:, rows + 1, 0], whole[:, :rows]))
    return pieces


def swap_cores(part):
    return lax.ppermute(part, "seq_2", [(0, 1), (1, 0)])


def ring_sum(part, axis):
    peers = lax.axis_size(axis)
    total = part
    for d in range(1, peers):
        total = total + lax.ppermute(part, axis, [(i, (i + d) % peers) for i in range(peers)])
    return total


def prefix_over(shifted, place):
    peers = len(shifted)
    own = shifted[0]
    start = nothing_yet(own, (1.0, 0.0))
    before, after = (start, start)
    for d in range(1, peers):
        taken = d <= place
        grown = link_states(shifted[d], before)
        before = jax.tree.map(lambda new, old: jnp.where(taken, new, old), grown, before)
    for d in range(peers - 1, 0, -1):
        taken = d > place
        grown = link_states(after, shifted[d])
        after = jax.tree.map(lambda new, old: jnp.where(taken, new, old), grown, after)
    return before, link_states(link_states(before, own), after)


def entering_state(decay, state):
    core = lax.axis_index("seq_2")
    half = decay.shape[0] // 2
    other_decay = swap_cores(decay)
    first_decay = jnp.where(core == 0, decay, other_decay)
    second_decay = jnp.where(core == 0, other_decay, decay)
    got = swap_cores(lax.dynamic_slice_in_dim(state, (1 - core) * half, half, 0))
    kept = lax.dynamic_slice_in_dim(state, core * half, half, 0)
    late = lax.ppermute(state[:half], "seq_2", [(0, 1)])
    first = (
        lax.dynamic_slice_in_dim(first_decay, core * half, half, 0),
        jnp.where(core == 0, kept, got),
    )
    second = (
        lax.dynamic_slice_in_dim(second_decay, core * half, half, 0),
        jnp.where(core == 0, got, kept),
    )
    mine = link_states(first, second)
    along_y, row = prefix_over(packed_shifts(*mine, "seq_1"), lax.axis_index("seq_1"))
    along_x, _ = prefix_over(packed_shifts(*row, "seq_0"), lax.axis_index("seq_0"))
    chip_before = link_states(along_x, along_y)[1]
    theirs = swap_cores(chip_before)
    whole = jnp.where(
        core == 0, jnp.concatenate([chip_before, theirs], 0), jnp.concatenate([theirs, chip_before], 0)
    )
    first_state = jnp.concatenate([late, got], 0)
    return jnp.where(core == 0, whole, first_decay[:, None, None] * whole + first_state)


def finish_rows(gate_sum, up_sum, squares):
    inv_rms = lax.rsqrt(squares / D + 1e-06)[None, :]
    return (jax.nn.silu(gate_sum * inv_rms) * (up_sum * inv_rms)).astype(jnp.bfloat16)


def body(
    query_rows,
    key_rows,
    value_rows,
    log_decay,
    out_weight,
    residual,
    routes,
    gate_weight,
    up_weight,
):
    positions, head_cols = query_rows.shape
    heads_here = head_cols // HEAD_DIM
    queries = query_rows.astype(jnp.float32).reshape(positions, heads_here, HEAD_DIM)
    keys_here = key_rows.astype(jnp.float32).reshape(positions, heads_here, HEAD_DIM)
    values_here = value_rows.astype(jnp.float32).reshape(positions, heads_here, HEAD_DIM)
    cumulative = jnp.cumsum(log_decay, axis=0)
    closing = cumulative[-1]
    key_scaled = keys_here * jnp.exp(closing[None, :] - cumulative)[:, :, None]
    local_state = jnp.einsum("shd,she->hde", key_scaled, values_here, precision=precise)
    entering = entering_state(jnp.exp(closing), local_state)
    later = lax.broadcasted_iota(jnp.int32, (positions, positions), 0)
    earlier = lax.broadcasted_iota(jnp.int32, (positions, positions), 1)
    causal = (later >= earlier)[None]
    carried = jnp.einsum(
        "thd,hde->the", queries * jnp.exp(cumulative)[:, :, None], entering, precision=precise
    )
    scores = jnp.einsum("thd,shd->hts", queries, keys_here, precision=precise)
    spread = cumulative.T[:, :, None] - cumulative.T[:, None, :]
    weights = jnp.where(causal, jnp.exp(jnp.where(causal, spread, 0.0)), 0.0)
    within = jnp.einsum("hts,she->the", scores * weights, values_here, precision=precise)
    head_raw = carried + within
    normed = head_raw * lax.rsqrt(jnp.mean(head_raw * head_raw, axis=-1, keepdims=True) + 1e-06)
    normed = normed.astype(jnp.bfloat16).reshape(positions, head_cols)
    gathered = lax.all_gather(normed, SEQ, axis=0, tiled=True)
    row_block = gathered
    attended = lax.psum_scatter(
        lax.dot_general(out_weight, row_block, (((0,), (1,)), ((), ())), preferred_element_type=jnp.float32),
        "exp",
        scatter_dimension=1,
        tiled=True,
    ).T
    residual_out = (residual.astype(jnp.float32) + attended).astype(jnp.bfloat16)
    group_rows = routes.shape[0]
    choices_each = routes.shape[1]
    experts = lax.axis_size("exp")
    capacity = 4 * group_rows // experts
    route_flat = routes.reshape(-1)
    expert_ids = lax.broadcasted_iota(jnp.int32, (1, experts), 1)
    onehot = (route_flat[:, None] == expert_ids).astype(jnp.int32)
    slot_index = jnp.sum(jnp.cumsum(onehot, axis=0) * onehot, axis=1) - 1
    target = route_flat * capacity + slot_index
    w_gate = gate_weight[0]
    w_up = up_weight[0]
    hidden_rows = w_gate.shape[0]
    columns = residual_out.shape[1]
    slots = lax.broadcasted_iota(jnp.int32, (experts * capacity, 1), 0)
    placed = target.reshape(group_rows, choices_each)
    picks = jnp.zeros((experts * capacity, group_rows), jnp.bool_)
    for j in range(choices_each):
        picks = picks | (slots == placed[None, :, j])
    buffer = jnp.dot(
        picks.astype(jnp.bfloat16), residual_out, preferred_element_type=jnp.float32
    ).astype(jnp.bfloat16)
    received = lax.all_to_all(
        buffer.reshape(experts, capacity, columns), "exp", split_axis=0, concat_axis=0, tiled=True
    )
    sources, entries, gathered_columns = received.shape
    slices = received.reshape(sources * entries, gathered_columns)
    row_block = lax.all_gather(slices, SEQ, axis=1, tiled=True)
    squares = jnp.einsum("rd,rd->r", slices, slices, preferred_element_type=jnp.float32)
    for axis in reversed(SEQ):
        squares = ring_sum(squares, axis)
    both = lax.dot_general(
        jnp.concatenate([w_gate, w_up], 0), row_block, contract_last, preferred_element_type=jnp.float32
    )
    gate_sum, up_sum = (both[:hidden_rows], both[hidden_rows:])
    expert_hidden = finish_rows(gate_sum, up_sum, squares).reshape(hidden_rows, sources, entries)
    return (residual_out, expert_hidden.reshape(1, hidden_rows, experts * capacity))


def solution(mesh):
    torus = Mesh(
        mesh.devices.reshape(4, 4, 2, mesh.shape["exp"]), ("seq_0", "seq_1", "seq_2", "exp")
    )
    in_specs = (
        P(SEQ, "exp"),
        P(SEQ, "exp"),
        P(SEQ, "exp"),
        P(SEQ, "exp"),
        P("exp", SEQ),
        P("exp", SEQ),
        P("exp", None),
        P("exp", SEQ, None),
        P("exp", SEQ, None),
    )
    out_specs = (P("exp", SEQ), P("exp", SEQ, None))
    return jax.shard_map(body, mesh=torus, in_specs=in_specs, out_specs=out_specs, check_vma=False)
```

```python
import jax
import jax.numpy as jnp
from jax import lax
from jax.sharding import Mesh
from jax.sharding import PartitionSpec as P

D = 6144
HEAD_DIM = 128
SEQ = ("seq_0", "seq_1", "seq_2")


precise = lax.Precision.HIGHEST
contract_last = (((1,), (1,)), ((), ()))


def nothing_yet(shard, identity):
    return jax.tree.map(
        lambda a, e: jnp.broadcast_to(jnp.asarray(e, a.dtype), a.shape), shard, identity
    )


def carried_in(shard, axes, combine, identity):
    before = start = nothing_yet(shard, identity)
    so_far = shard
    for axis in reversed(axes):
        peers, place = (lax.axis_size(axis), lax.axis_index(axis))
        pieces = jax.tree.map(lambda part: lax.all_gather(part, axis), so_far)
        inside, so_far = (start, start)
        for k in range(peers):
            passed = k < place
            so_far = combine(so_far, jax.tree.map(lambda part: part[k], pieces))
            inside = jax.tree.map(lambda new, old: jnp.where(passed, new, old), so_far, inside)
        before = combine(inside, before)
    return before


def link_states(earlier, later):
    return (earlier[0] * later[0], later[0][:, None, None] * earlier[1] + later[1])


def ring_shifts(part, axis):
    peers = lax.axis_size(axis)
    return [part] + [
        lax.ppermute(part, axis, [(i, (i + d) % peers) for i in range(peers)]) for d in range(1, peers)
    ]


def packed_shifts(decay, state, axis):
    heads, rows, cols = state.shape
    scaled = decay * 65537.0
    leading = scaled - (scaled - decay)
    high = leading.astype(jnp.bfloat16)
    low = (decay - leading).astype(jnp.bfloat16)
    tail = jnp.concatenate(
        [
            jnp.broadcast_to(high[:, None, None], (heads, 1, cols)),
            jnp.broadcast_to(low[:, None, None], (heads, 1, cols)),
            jnp.zeros((heads, 6, cols), jnp.bfloat16),
        ],
        axis=1,
    )
    packed = jnp.concatenate([state.astype(jnp.bfloat16), tail], axis=1)
    pieces = [(decay, state)]
    for moved in ring_shifts(packed, axis)[1:]:
        whole = moved.astype(jnp.float32)
        pieces.append((whole[:, rows, 0] + whole[:, rows + 1, 0], whole[:, :rows]))
    return pieces


def swap_cores(part):
    return lax.ppermute(part, "seq_2", [(0, 1), (1, 0)])


def ring_sum(part, axis):
    peers = lax.axis_size(axis)
    total = part
    for d in range(1, peers):
        total = total + lax.ppermute(part, axis, [(i, (i + d) % peers) for i in range(peers)])
    return total


def prefix_over(shifted, place):
    peers = len(shifted)
    own = shifted[0]
    start = nothing_yet(own, (1.0, 0.0))
    before, after = (start, start)
    for d in range(1, peers):
        taken = d <= place
        grown = link_states(shifted[d], before)
        before = jax.tree.map(lambda new, old: jnp.where(taken, new, old), grown, before)
    for d in range(peers - 1, 0, -1):
        taken = d > place
        grown = link_states(after, shifted[d])
        after = jax.tree.map(lambda new, old: jnp.where(taken, new, old), grown, after)
    return before, link_states(link_states(before, own), after)


def entering_state(decay, state):
    core = lax.axis_index("seq_2")
    half = decay.shape[0] // 2
    other = (swap_cores(decay), swap_cores(state))
    first = jax.tree.map(lambda mine, theirs: jnp.where(core == 0, mine, theirs), (decay, state), other)
    second = jax.tree.map(lambda mine, theirs: jnp.where(core == 0, theirs, mine), (decay, state), other)
    chip = link_states(first, second)
    mine = jax.tree.map(lambda part: lax.dynamic_slice_in_dim(part, core * half, half, 0), chip)
    along_y, row = prefix_over(packed_shifts(*mine, "seq_1"), lax.axis_index("seq_1"))
    along_x, _ = prefix_over(packed_shifts(*row, "seq_0"), lax.axis_index("seq_0"))
    chip_before = link_states(along_x, along_y)[1]
    theirs = swap_cores(chip_before)

    def finish(part, start):
        decay_part = lax.dynamic_slice_in_dim(first[0], start, half, 0)
        state_part = lax.dynamic_slice_in_dim(first[1], start, half, 0)
        return jnp.where(core == 0, part, decay_part[:, None, None] * part + state_part)

    return (finish(chip_before, core * half), finish(theirs, (1 - core) * half))


def finish_rows(gate_sum, up_sum, squares):
    inv_rms = lax.rsqrt(squares / D + 1e-06)[None, :]
    return (jax.nn.silu(gate_sum * inv_rms) * (up_sum * inv_rms)).astype(jnp.bfloat16)


def body(
    query_rows,
    key_rows,
    value_rows,
    log_decay,
    out_weight,
    residual,
    routes,
    gate_weight,
    up_weight,
):
    positions, head_cols = query_rows.shape
    heads_here = head_cols // HEAD_DIM
    queries = query_rows.astype(jnp.float32).reshape(positions, heads_here, HEAD_DIM)
    keys_here = key_rows.astype(jnp.float32).reshape(positions, heads_here, HEAD_DIM)
    values_here = value_rows.astype(jnp.float32).reshape(positions, heads_here, HEAD_DIM)
    cumulative = jnp.cumsum(log_decay, axis=0)
    closing = cumulative[-1]
    key_scaled = keys_here * jnp.exp(closing[None, :] - cumulative)[:, :, None]
    local_state = jnp.einsum("shd,she->hde", key_scaled, values_here, precision=precise)
    own_heads, other_heads = entering_state(jnp.exp(closing), local_state)
    later = lax.broadcasted_iota(jnp.int32, (positions, positions), 0)
    earlier = lax.broadcasted_iota(jnp.int32, (positions, positions), 1)
    causal = (later >= earlier)[None]
    core = lax.axis_index("seq_2")
    half = heads_here // 2
    scaled = queries * jnp.exp(cumulative)[:, :, None]

    def carry(part, start):
        block = lax.dynamic_slice_in_dim(scaled, start, half, 1)
        return jnp.einsum("thd,hde->the", block, part, precision=precise)

    own_carried = carry(own_heads, core * half)
    other_carried = carry(other_heads, (1 - core) * half)
    carried = jnp.where(
        core == 0,
        jnp.concatenate([own_carried, other_carried], 1),
        jnp.concatenate([other_carried, own_carried], 1),
    )
    scores = jnp.einsum("thd,shd->hts", queries, keys_here, precision=precise)
    spread = cumulative.T[:, :, None] - cumulative.T[:, None, :]
    weights = jnp.where(causal, jnp.exp(jnp.where(causal, spread, 0.0)), 0.0)
    within = jnp.einsum("hts,she->the", scores * weights, values_here, precision=precise)
    head_raw = carried + within
    normed = head_raw * lax.rsqrt(jnp.mean(head_raw * head_raw, axis=-1, keepdims=True) + 1e-06)
    normed = normed.astype(jnp.bfloat16).reshape(positions, head_cols)
    gathered = lax.all_gather(normed, SEQ, axis=0, tiled=True)
    row_block = gathered
    attended = lax.psum_scatter(
        lax.dot_general(out_weight, row_block, (((0,), (1,)), ((), ())), preferred_element_type=jnp.float32),
        "exp",
        scatter_dimension=1,
        tiled=True,
    ).T
    residual_out = (residual.astype(jnp.float32) + attended).astype(jnp.bfloat16)
    group_rows = routes.shape[0]
    choices_each = routes.shape[1]
    experts = lax.axis_size("exp")
    capacity = 4 * group_rows // experts
    route_flat = routes.reshape(-1)
    expert_ids = lax.broadcasted_iota(jnp.int32, (1, experts), 1)
    onehot = (route_flat[:, None] == expert_ids).astype(jnp.int32)
    slot_index = jnp.sum(jnp.cumsum(onehot, axis=0) * onehot, axis=1) - 1
    target = route_flat * capacity + slot_index
    w_gate = gate_weight[0]
    w_up = up_weight[0]
    hidden_rows = w_gate.shape[0]
    columns = residual_out.shape[1]
    slots = lax.broadcasted_iota(jnp.int32, (experts * capacity, 1), 0)
    placed = target.reshape(group_rows, choices_each)
    picks = jnp.zeros((experts * capacity, group_rows), jnp.bool_)
    for j in range(choices_each):
        picks = picks | (slots == placed[None, :, j])
    buffer = jnp.dot(
        picks.astype(jnp.bfloat16), residual_out, preferred_element_type=jnp.float32
    ).astype(jnp.bfloat16)
    received = lax.all_to_all(
        buffer.reshape(experts, capacity, columns), "exp", split_axis=0, concat_axis=0, tiled=True
    )
    sources, entries, gathered_columns = received.shape
    slices = received.reshape(sources * entries, gathered_columns)
    row_block = lax.all_gather(slices, SEQ, axis=1, tiled=True)
    squares = jnp.einsum("rd,rd->r", slices, slices, preferred_element_type=jnp.float32)
    for axis in reversed(SEQ):
        squares = ring_sum(squares, axis)
    both = lax.dot_general(
        jnp.concatenate([w_gate, w_up], 0), row_block, contract_last, preferred_element_type=jnp.float32
    )
    gate_sum, up_sum = (both[:hidden_rows], both[hidden_rows:])
    expert_hidden = finish_rows(gate_sum, up_sum, squares).reshape(hidden_rows, sources, entries)
    return (residual_out, expert_hidden.reshape(1, hidden_rows, experts * capacity))


def solution(mesh):
    torus = Mesh(
        mesh.devices.reshape(4, 4, 2, mesh.shape["exp"]), ("seq_0", "seq_1", "seq_2", "exp")
    )
    in_specs = (
        P(SEQ, "exp"),
        P(SEQ, "exp"),
        P(SEQ, "exp"),
        P(SEQ, "exp"),
        P("exp", SEQ),
        P("exp", SEQ),
        P("exp", None),
        P("exp", SEQ, None),
        P("exp", SEQ, None),
    )
    out_specs = (P("exp", SEQ), P("exp", SEQ, None))
    return jax.shard_map(body, mesh=torus, in_specs=in_specs, out_specs=out_specs, check_vma=False)
```

```python
import jax
import jax.numpy as jnp
from jax import lax
from jax.sharding import Mesh
from jax.sharding import PartitionSpec as P

D = 6144
HEAD_DIM = 128
SEQ = ("seq_0", "seq_1", "seq_2")


precise = lax.Precision.HIGHEST
contract_last = (((1,), (1,)), ((), ()))


def nothing_yet(shard, identity):
    return jax.tree.map(
        lambda a, e: jnp.broadcast_to(jnp.asarray(e, a.dtype), a.shape), shard, identity
    )


def carried_in(shard, axes, combine, identity):
    before = start = nothing_yet(shard, identity)
    so_far = shard
    for axis in reversed(axes):
        peers, place = (lax.axis_size(axis), lax.axis_index(axis))
        pieces = jax.tree.map(lambda part: lax.all_gather(part, axis), so_far)
        inside, so_far = (start, start)
        for k in range(peers):
            passed = k < place
            so_far = combine(so_far, jax.tree.map(lambda part: part[k], pieces))
            inside = jax.tree.map(lambda new, old: jnp.where(passed, new, old), so_far, inside)
        before = combine(inside, before)
    return before


def link_states(earlier, later):
    return (earlier[0] * later[0], later[0][:, None, None] * earlier[1] + later[1])


def ring_shifts(part, axis):
    peers = lax.axis_size(axis)
    return [part] + [
        lax.ppermute(part, axis, [(i, (i + d) % peers) for i in range(peers)]) for d in range(1, peers)
    ]


def packed_shifts(decay, state, axis):
    heads, rows, cols = state.shape
    scaled = decay * 65537.0
    leading = scaled - (scaled - decay)
    high = leading.astype(jnp.bfloat16)
    low = (decay - leading).astype(jnp.bfloat16)
    tail = jnp.concatenate(
        [
            jnp.broadcast_to(high[:, None, None], (heads, 1, cols)),
            jnp.broadcast_to(low[:, None, None], (heads, 1, cols)),
            jnp.zeros((heads, 6, cols), jnp.bfloat16),
        ],
        axis=1,
    )
    packed = jnp.concatenate([state.astype(jnp.bfloat16), tail], axis=1)
    pieces = [(decay, state)]
    for moved in ring_shifts(packed, axis)[1:]:
        whole = moved.astype(jnp.float32)
        pieces.append((whole[:, rows, 0] + whole[:, rows + 1, 0], whole[:, :rows]))
    return pieces


def swap_cores(part):
    return lax.ppermute(part, "seq_2", [(0, 1), (1, 0)])


def ring_sum(part, axis):
    peers = lax.axis_size(axis)
    total = part
    for d in range(1, peers):
        total = total + lax.ppermute(part, axis, [(i, (i + d) % peers) for i in range(peers)])
    return total


def prefix_over(shifted, place):
    peers = len(shifted)
    own = shifted[0]
    start = nothing_yet(own, (1.0, 0.0))
    before, after = (start, start)
    for d in range(1, peers):
        taken = d <= place
        grown = link_states(shifted[d], before)
        before = jax.tree.map(lambda new, old: jnp.where(taken, new, old), grown, before)
    for d in range(peers - 1, 0, -1):
        taken = d > place
        grown = link_states(after, shifted[d])
        after = jax.tree.map(lambda new, old: jnp.where(taken, new, old), grown, after)
    return before, link_states(link_states(before, own), after)


def entering_state(decay, state):
    core = lax.axis_index("seq_2")
    half = decay.shape[0] // 2
    other = (swap_cores(decay), swap_cores(state))
    first = jax.tree.map(lambda mine, theirs: jnp.where(core == 0, mine, theirs), (decay, state), other)
    second = jax.tree.map(lambda mine, theirs: jnp.where(core == 0, theirs, mine), (decay, state), other)
    chip = link_states(first, second)
    mine = jax.tree.map(lambda part: lax.dynamic_slice_in_dim(part, core * half, half, 0), chip)
    along_y, row = prefix_over(packed_shifts(*mine, "seq_1"), lax.axis_index("seq_1"))
    along_x, _ = prefix_over(packed_shifts(*row, "seq_0"), lax.axis_index("seq_0"))
    chip_before = link_states(along_x, along_y)[1]
    theirs = swap_cores(chip_before)
    whole = jnp.where(
        core == 0, jnp.concatenate([chip_before, theirs], 0), jnp.concatenate([theirs, chip_before], 0)
    )
    return jnp.where(core == 0, whole, first[0][:, None, None] * whole + first[1])


def finish_rows(gate_sum, up_sum, squares):
    inv_rms = lax.rsqrt(squares / D + 1e-06)[None, :]
    return (jax.nn.silu(gate_sum * inv_rms) * (up_sum * inv_rms)).astype(jnp.bfloat16)


def body(
    query_rows,
    key_rows,
    value_rows,
    log_decay,
    out_weight,
    residual,
    routes,
    gate_weight,
    up_weight,
):
    positions, head_cols = query_rows.shape
    heads_here = head_cols // HEAD_DIM
    queries = query_rows.astype(jnp.float32).reshape(positions, heads_here, HEAD_DIM)
    keys_here = key_rows.astype(jnp.float32).reshape(positions, heads_here, HEAD_DIM)
    values_here = value_rows.astype(jnp.float32).reshape(positions, heads_here, HEAD_DIM)
    cumulative = jnp.cumsum(log_decay, axis=0)
    closing = cumulative[-1]
    key_scaled = keys_here * jnp.exp(closing[None, :] - cumulative)[:, :, None]
    local_state = jnp.einsum("shd,she->hde", key_scaled, values_here, precision=precise)
    entering = entering_state(jnp.exp(closing), local_state)
    later = lax.broadcasted_iota(jnp.int32, (positions, positions), 0)
    earlier = lax.broadcasted_iota(jnp.int32, (positions, positions), 1)
    causal = (later >= earlier)[None]
    carried = jnp.einsum(
        "thd,hde->the", queries * jnp.exp(cumulative)[:, :, None], entering, precision=precise
    )
    scores = jnp.einsum("thd,shd->hts", queries, keys_here, precision=precise)
    spread = cumulative.T[:, :, None] - cumulative.T[:, None, :]
    weights = jnp.where(causal, jnp.exp(jnp.where(causal, spread, 0.0)), 0.0)
    within = jnp.einsum("hts,she->the", scores * weights, values_here, precision=precise)
    head_raw = carried + within
    normed = head_raw * lax.rsqrt(jnp.mean(head_raw * head_raw, axis=-1, keepdims=True) + 1e-06)
    normed = normed.astype(jnp.bfloat16).reshape(positions, head_cols)
    gathered = lax.all_gather(normed, SEQ, axis=0, tiled=True)
    row_block = gathered
    attended = lax.psum_scatter(
        lax.dot_general(
            out_weight, row_block, (((0,), (1,)), ((), ())), preferred_element_type=jnp.float32
        ).astype(jnp.bfloat16),
        "exp",
        scatter_dimension=1,
        tiled=True,
    ).T.astype(jnp.float32)
    residual_out = (residual.astype(jnp.float32) + attended).astype(jnp.bfloat16)
    group_rows = routes.shape[0]
    choices_each = routes.shape[1]
    experts = lax.axis_size("exp")
    capacity = 4 * group_rows // experts
    route_flat = routes.reshape(-1)
    expert_ids = lax.broadcasted_iota(jnp.int32, (1, experts), 1)
    onehot = (route_flat[:, None] == expert_ids).astype(jnp.int32)
    slot_index = jnp.sum(jnp.cumsum(onehot, axis=0) * onehot, axis=1) - 1
    target = route_flat * capacity + slot_index
    w_gate = gate_weight[0]
    w_up = up_weight[0]
    hidden_rows = w_gate.shape[0]
    columns = residual_out.shape[1]
    slots = lax.broadcasted_iota(jnp.int32, (experts * capacity, 1), 0)
    placed = target.reshape(group_rows, choices_each)
    picks = jnp.zeros((experts * capacity, group_rows), jnp.bool_)
    for j in range(choices_each):
        picks = picks | (slots == placed[None, :, j])
    buffer = jnp.dot(
        picks.astype(jnp.bfloat16), residual_out, preferred_element_type=jnp.float32
    ).astype(jnp.bfloat16)
    received = lax.all_to_all(
        buffer.reshape(experts, capacity, columns), "exp", split_axis=0, concat_axis=0, tiled=True
    )
    sources, entries, gathered_columns = received.shape
    slices = received.reshape(sources * entries, gathered_columns)
    row_block = lax.all_gather(slices, SEQ, axis=1, tiled=True)
    squares = jnp.einsum("rd,rd->r", slices, slices, preferred_element_type=jnp.float32)
    for axis in reversed(SEQ):
        squares = ring_sum(squares, axis)
    both = lax.dot_general(
        jnp.concatenate([w_gate, w_up], 0), row_block, contract_last, preferred_element_type=jnp.float32
    )
    gate_sum, up_sum = (both[:hidden_rows], both[hidden_rows:])
    expert_hidden = finish_rows(gate_sum, up_sum, squares).reshape(hidden_rows, sources, entries)
    return (residual_out, expert_hidden.reshape(1, hidden_rows, experts * capacity))


def solution(mesh):
    torus = Mesh(
        mesh.devices.reshape(4, 4, 2, mesh.shape["exp"]), ("seq_0", "seq_1", "seq_2", "exp")
    )
    in_specs = (
        P(SEQ, "exp"),
        P(SEQ, "exp"),
        P(SEQ, "exp"),
        P(SEQ, "exp"),
        P("exp", SEQ),
        P("exp", SEQ),
        P("exp", None),
        P("exp", SEQ, None),
        P("exp", SEQ, None),
    )
    out_specs = (P("exp", SEQ), P("exp", SEQ, None))
    return jax.shard_map(body, mesh=torus, in_specs=in_specs, out_specs=out_specs, check_vma=False)
```

```python
import jax
import jax.numpy as jnp
from jax import lax
from jax.sharding import Mesh
from jax.sharding import PartitionSpec as P

D = 6144
HEAD_DIM = 128
SEQ = ("seq_0", "seq_1", "seq_2")


precise = lax.Precision.HIGHEST
contract_last = (((1,), (1,)), ((), ()))


def nothing_yet(shard, identity):
    return jax.tree.map(
        lambda a, e: jnp.broadcast_to(jnp.asarray(e, a.dtype), a.shape), shard, identity
    )


def carried_in(shard, axes, combine, identity):
    before = start = nothing_yet(shard, identity)
    so_far = shard
    for axis in reversed(axes):
        peers, place = (lax.axis_size(axis), lax.axis_index(axis))
        pieces = jax.tree.map(lambda part: lax.all_gather(part, axis), so_far)
        inside, so_far = (start, start)
        for k in range(peers):
            passed = k < place
            so_far = combine(so_far, jax.tree.map(lambda part: part[k], pieces))
            inside = jax.tree.map(lambda new, old: jnp.where(passed, new, old), so_far, inside)
        before = combine(inside, before)
    return before


def link_states(earlier, later):
    return (earlier[0] * later[0], later[0][:, None, None] * earlier[1] + later[1])


def ring_shifts(part, axis):
    peers = lax.axis_size(axis)
    return [part] + [
        lax.ppermute(part, axis, [(i, (i + d) % peers) for i in range(peers)]) for d in range(1, peers)
    ]


def packed_shifts(decay, state, axis):
    heads, rows, cols = state.shape
    scaled = decay * 65537.0
    leading = scaled - (scaled - decay)
    high = leading.astype(jnp.bfloat16)
    low = (decay - leading).astype(jnp.bfloat16)
    tail = jnp.concatenate(
        [
            jnp.broadcast_to(high[:, None, None], (heads, 1, cols)),
            jnp.broadcast_to(low[:, None, None], (heads, 1, cols)),
            jnp.zeros((heads, 6, cols), jnp.bfloat16),
        ],
        axis=1,
    )
    packed = jnp.concatenate([state.astype(jnp.bfloat16), tail], axis=1)
    pieces = [(decay, state)]
    for moved in ring_shifts(packed, axis)[1:]:
        whole = moved.astype(jnp.float32)
        pieces.append((whole[:, rows, 0] + whole[:, rows + 1, 0], whole[:, :rows]))
    return pieces


def swap_cores(part):
    return lax.ppermute(part, "seq_2", [(0, 1), (1, 0)])


def ring_sum(part, axis):
    peers = lax.axis_size(axis)
    total = part
    for d in range(1, peers):
        total = total + lax.ppermute(part, axis, [(i, (i + d) % peers) for i in range(peers)])
    return total


def prefix_over(shifted, place):
    peers = len(shifted)
    own = shifted[0]
    start = nothing_yet(own, (1.0, 0.0))
    before, after = (start, start)
    for d in range(1, peers):
        taken = d <= place
        grown = link_states(shifted[d], before)
        before = jax.tree.map(lambda new, old: jnp.where(taken, new, old), grown, before)
    for d in range(peers - 1, 0, -1):
        taken = d > place
        grown = link_states(after, shifted[d])
        after = jax.tree.map(lambda new, old: jnp.where(taken, new, old), grown, after)
    return before, link_states(link_states(before, own), after)


def entering_state(decay, state):
    core = lax.axis_index("seq_2")
    half = decay.shape[0] // 2
    other = (swap_cores(decay), swap_cores(state))
    first = jax.tree.map(lambda mine, theirs: jnp.where(core == 0, mine, theirs), (decay, state), other)
    second = jax.tree.map(lambda mine, theirs: jnp.where(core == 0, theirs, mine), (decay, state), other)
    chip = link_states(first, second)
    mine = jax.tree.map(lambda part: lax.dynamic_slice_in_dim(part, core * half, half, 0), chip)
    along_y, row = prefix_over(packed_shifts(*mine, "seq_1"), lax.axis_index("seq_1"))
    along_x, _ = prefix_over(packed_shifts(*row, "seq_0"), lax.axis_index("seq_0"))
    chip_before = link_states(along_x, along_y)[1]
    theirs = swap_cores(chip_before.astype(jnp.bfloat16)).astype(jnp.float32)
    whole = jnp.where(
        core == 0, jnp.concatenate([chip_before, theirs], 0), jnp.concatenate([theirs, chip_before], 0)
    )
    return jnp.where(core == 0, whole, first[0][:, None, None] * whole + first[1])


def finish_rows(gate_sum, up_sum, squares):
    inv_rms = lax.rsqrt(squares / D + 1e-06)[None, :]
    return (jax.nn.silu(gate_sum * inv_rms) * (up_sum * inv_rms)).astype(jnp.bfloat16)


def body(
    query_rows,
    key_rows,
    value_rows,
    log_decay,
    out_weight,
    residual,
    routes,
    gate_weight,
    up_weight,
):
    positions, head_cols = query_rows.shape
    heads_here = head_cols // HEAD_DIM
    queries = query_rows.astype(jnp.float32).reshape(positions, heads_here, HEAD_DIM)
    keys_here = key_rows.astype(jnp.float32).reshape(positions, heads_here, HEAD_DIM)
    values_here = value_rows.astype(jnp.float32).reshape(positions, heads_here, HEAD_DIM)
    cumulative = jnp.cumsum(log_decay, axis=0)
    closing = cumulative[-1]
    key_scaled = keys_here * jnp.exp(closing[None, :] - cumulative)[:, :, None]
    local_state = jnp.einsum("shd,she->hde", key_scaled, values_here, precision=precise)
    entering = entering_state(jnp.exp(closing), local_state)
    later = lax.broadcasted_iota(jnp.int32, (positions, positions), 0)
    earlier = lax.broadcasted_iota(jnp.int32, (positions, positions), 1)
    causal = (later >= earlier)[None]
    carried = jnp.einsum(
        "thd,hde->the", queries * jnp.exp(cumulative)[:, :, None], entering, precision=precise
    )
    scores = jnp.einsum("thd,shd->hts", queries, keys_here, precision=precise)
    spread = cumulative.T[:, :, None] - cumulative.T[:, None, :]
    weights = jnp.where(causal, jnp.exp(jnp.where(causal, spread, 0.0)), 0.0)
    within = jnp.einsum("hts,she->the", scores * weights, values_here, precision=precise)
    head_raw = carried + within
    normed = head_raw * lax.rsqrt(jnp.mean(head_raw * head_raw, axis=-1, keepdims=True) + 1e-06)
    normed = normed.astype(jnp.bfloat16).reshape(positions, head_cols)
    gathered = lax.all_gather(normed, SEQ, axis=0, tiled=True)
    row_block = gathered
    attended = lax.psum_scatter(
        lax.dot_general(out_weight, row_block, (((0,), (1,)), ((), ())), preferred_element_type=jnp.float32),
        "exp",
        scatter_dimension=1,
        tiled=True,
    ).T
    residual_out = (residual.astype(jnp.float32) + attended).astype(jnp.bfloat16)
    group_rows = routes.shape[0]
    choices_each = routes.shape[1]
    experts = lax.axis_size("exp")
    capacity = 4 * group_rows // experts
    route_flat = routes.reshape(-1)
    expert_ids = lax.broadcasted_iota(jnp.int32, (1, experts), 1)
    onehot = (route_flat[:, None] == expert_ids).astype(jnp.int32)
    slot_index = jnp.sum(jnp.cumsum(onehot, axis=0) * onehot, axis=1) - 1
    target = route_flat * capacity + slot_index
    w_gate = gate_weight[0]
    w_up = up_weight[0]
    hidden_rows = w_gate.shape[0]
    columns = residual_out.shape[1]
    slots = lax.broadcasted_iota(jnp.int32, (experts * capacity, 1), 0)
    placed = target.reshape(group_rows, choices_each)
    picks = jnp.zeros((experts * capacity, group_rows), jnp.bool_)
    for j in range(choices_each):
        picks = picks | (slots == placed[None, :, j])
    buffer = jnp.dot(
        picks.astype(jnp.bfloat16), residual_out, preferred_element_type=jnp.float32
    ).astype(jnp.bfloat16)
    received = lax.all_to_all(
        buffer.reshape(experts, capacity, columns), "exp", split_axis=0, concat_axis=0, tiled=True
    )
    sources, entries, gathered_columns = received.shape
    slices = received.reshape(sources * entries, gathered_columns)
    row_block = lax.all_gather(slices, SEQ, axis=1, tiled=True)
    squares = jnp.einsum("rd,rd->r", slices, slices, preferred_element_type=jnp.float32)
    for axis in reversed(SEQ):
        squares = ring_sum(squares, axis)
    both = lax.dot_general(
        jnp.concatenate([w_gate, w_up], 0), row_block, contract_last, preferred_element_type=jnp.float32
    )
    gate_sum, up_sum = (both[:hidden_rows], both[hidden_rows:])
    expert_hidden = finish_rows(gate_sum, up_sum, squares).reshape(hidden_rows, sources, entries)
    return (residual_out, expert_hidden.reshape(1, hidden_rows, experts * capacity))


def solution(mesh):
    torus = Mesh(
        mesh.devices.reshape(4, 4, 2, mesh.shape["exp"]), ("seq_0", "seq_1", "seq_2", "exp")
    )
    in_specs = (
        P(SEQ, "exp"),
        P(SEQ, "exp"),
        P(SEQ, "exp"),
        P(SEQ, "exp"),
        P("exp", SEQ),
        P("exp", SEQ),
        P("exp", None),
        P("exp", SEQ, None),
        P("exp", SEQ, None),
    )
    out_specs = (P("exp", SEQ), P("exp", SEQ, None))
    return jax.shard_map(body, mesh=torus, in_specs=in_specs, out_specs=out_specs, check_vma=False)
```
